256 devices in a mesh: gx: 32 (over x, y, core), gy: 8 (over z).
Axes of the slice: x: 4, y: 4, z: 8, core: 2. Of those that a mesh axis runs over, the one named last changes fastest.
Arguments:
- leaf_load: bfloat16 [65536, 384], P(('gx', 'gy')), may hold values from -6 to 6
- front_zero: bfloat16 [65536, 8192], P(('gx', 'gy')), may hold values from -0.046875 to 0.046875
- front_one: bfloat16 [32768, 8192], P(('gx', 'gy')), may hold values from -0.046875 to 0.046875
- front_two: bfloat16 [16384, 8192], P(('gx', 'gy')), may hold values from -0.046875 to 0.046875
- front_root: bfloat16 [8192, 8192], P(('gx', 'gy')), may hold values from -0.046875 to 0.046875
- load_one: float32 [32768, 384], P(('gx', 'gy')), may hold values from -6 to 6
- load_two: float32 [16384, 384], P(('gx', 'gy')), may hold values from -6 to 6
- load_root: float32 [8192, 384], P(('gx', 'gy')), may hold values from -6 to 6
- map_one: int32 [8192, 2], replicated, may hold values from 0 to 255
- map_two: int32 [8192, 2], replicated, may hold values from 0 to 127
- map_root: int32 [8192, 2], replicated, may hold values from 0 to 63
- adjoint: float32 [64, 128, 384], P('gx', 'gy'), may hold values from -6 to 6
Outputs:
- root_solution: float32 [8192, 384], P(('gx', 'gy'))
- gradient: float32 [64, 128, 384], P('gx', 'gy')
The draws below stay inside these ranges and needn't reach their ends.
All inputs are finite; a program needn't handle non-finite values.
Results may differ from the reference program's by a relative error of at most 0.0055.
Values may be sent and summed in bfloat16 or wider, within the bound.
No kernel may reach another device: no remote copies, remote signals or barrier semaphores. Data moves between devices by JAX's collectives and lax.ppermute only.
A program may use at most 64 MiB of HBM per device.

```python
import jax
import jax.numpy as jnp
from jax import lax

FRONT = 8192
CASES = 384
LEAF_BITS = 2
ROWS0 = 256
PY = 16
PX = 2
NX = 64
NY = 128
N_GX = 32
N_GY = 8


def touch_ends(result, stream_key, least, top_value):
    spot = [jax.random.randint(jax.random.fold_in(stream_key, axis), (), 0, length) for axis, length in enumerate(result.shape)]
    widest = result.shape.index(max(result.shape))
    neighbour = spot[:widest] + [(spot[widest] + 1) % result.shape[widest]] + spot[widest + 1:]
    return result.at[tuple(spot)].set(least).at[tuple(neighbour)].set(top_value)


def block_levels(own_key, dims, cuts, low, high):
    gain, own = 1.0, jax.random.fold_in(own_key, 6)
    for axis_at, blocks in cuts:
        heights = jnp.exp(jax.random.uniform(jax.random.fold_in(own, axis_at), (blocks,), jnp.float32, low / len(cuts), high / len(cuts)))
        gain = gain * jnp.repeat(heights, dims[axis_at] // blocks).reshape([-1 if axis == axis_at else 1 for axis in range(len(dims))])
    return gain


def centred(key, shape, width, most, pieces=(), held_as=jnp.bfloat16):
    result = jax.random.normal(key, shape, jnp.float32) * width
    if len(pieces) > 0:
        result = block_levels(key, shape, pieces, -0.22, 0.18) * result
    return jnp.clip(result, min=-most, max=most).astype(held_as)


def setup_inputs(seed: int = 0) -> dict:
    keys = jax.random.split(jax.random.key(seed), 13)
    return {
        "leaf_load": centred(keys[0], (8 * FRONT, CASES), 1.0, 6.0, ((0, 256),)),
        "front_zero": centred(keys[1], (8 * FRONT, FRONT), (2 * FRONT) ** -0.5, 0.046875, ((0, 256),)),
        "front_one": centred(keys[2], (4 * FRONT, FRONT), (2 * FRONT) ** -0.5, 0.046875, ((0, 256),)),
        "front_two": centred(keys[3], (2 * FRONT, FRONT), (2 * FRONT) ** -0.5, 0.046875, ((0, 256),)),
        "front_root": centred(keys[4], (FRONT, FRONT), (2 * FRONT) ** -0.5, 0.046875, ((0, 256),)),
        "load_one": centred(keys[5], (4 * FRONT, CASES), 1.0, 6.0, ((0, 256),), jnp.float32),
        "load_two": centred(keys[6], (2 * FRONT, CASES), 1.0, 6.0, ((0, 256),), jnp.float32),
        "load_root": centred(keys[7], (FRONT, CASES), 1.0, 6.0, ((0, 256),), jnp.float32),
        "map_one": touch_ends(jax.random.randint(keys[8], (FRONT, 2), 0, ROWS0), jax.random.fold_in(keys[8], 1), 0, ROWS0 - 1).astype(jnp.int32),
        "map_two": touch_ends(jax.random.randint(keys[9], (FRONT, 2), 0, ROWS0 // 2), jax.random.fold_in(keys[9], 1), 0, (ROWS0 // 2) - 1).astype(jnp.int32),
        "map_root": touch_ends(jax.random.randint(keys[10], (FRONT, 2), 0, ROWS0 // 4), jax.random.fold_in(keys[10], 1), 0, (ROWS0 // 4) - 1).astype(jnp.int32),
        "adjoint": centred(keys[11], (NX, NY, CASES), 1.0, 6.0, ((0, 32), (1, 8)), jnp.float32),
    }


def apply_level(front, state):
    count = front.shape[0] // FRONT
    blocks = front.reshape(count, FRONT, FRONT)
    values = state.reshape(count, FRONT, CASES)
    product = lax.map(lambda pair: jnp.dot(pair[0], pair[1], preferred_element_type=jnp.float32), (blocks, values))
    return product.reshape(count * FRONT, CASES)


def extend(product, load, mapping, level):
    bit = LEAF_BITS + level
    span = 2 ** bit
    rows = product.shape[0] // (N_GX * N_GY)
    half = rows // 2
    outer = N_GX // (2 * span)
    full = (outer, 2, span, N_GY, rows, CASES)
    shape = (outer, 2, span, N_GY, half, CASES)
    six = product.reshape(full)
    first = jnp.broadcast_to(six[:, 0:1], full)
    second = jnp.broadcast_to(six[:, 1:2], full)
    index = mapping.reshape(1, 2, span, N_GY, half, 2).astype(jnp.int32)
    index_a = jnp.broadcast_to(index[..., 0:1], shape)
    index_b = jnp.broadcast_to(index[..., 1:2], shape)
    picked_a = jnp.take_along_axis(first, index_a, axis=4)
    picked_b = jnp.take_along_axis(second, index_b, axis=4)
    total = load.reshape(shape) + picked_a + picked_b
    return total.astype(jnp.bfloat16).reshape(outer * 2 * span * N_GY * half, CASES)


def reference(leaf_load, front_zero, front_one, front_two, front_root, load_one, load_two, load_root, map_one, map_two, map_root, adjoint):
    fronts = (front_zero, front_one, front_two, front_root)
    loads = (load_one, load_two, load_root)
    mappings = (map_one, map_two, map_root)
    state = leaf_load
    for level in range(3):
        product = apply_level(fronts[level], state)
        state = extend(product, loads[level], mappings[level], level)
    root_solution = apply_level(front_root, state)
    plane = root_solution.reshape(N_GX, N_GY, PX, PY, CASES).transpose(0, 2, 1, 3, 4).reshape(NX, NY, CASES)
    padded_u = jnp.pad(plane, ((1, 1), (1, 1), (0, 0)))
    padded_a = jnp.pad(adjoint, ((1, 1), (1, 1), (0, 0)))
    gradient = jnp.zeros((NX, NY, CASES), jnp.float32)
    for lo_x, lo_y in ((2, 1), (0, 1), (1, 2), (1, 0)):
        near_u = padded_u[lo_x:lo_x + NX, lo_y:lo_y + NY]
        near_a = padded_a[lo_x:lo_x + NX, lo_y:lo_y + NY]
        gradient = gradient + (plane - near_u) * (adjoint - near_a)
    return root_solution, gradient
```

```python
import numpy as np
import jax
import jax.numpy as jnp
from jax import lax
from jax.sharding import Mesh, PartitionSpec as P

GX = ("xa", "ya", "c")
ALL = ("xa", "ya", "c", "gy")


def moved(x, axis, pairs):
    return lax.ppermute(x, axis, pairs)


def ring_blocks(x, axis, n, size):
    if n == 2 and size != 2:
        return jnp.stack([x, moved(x, axis, [(i, i ^ 1) for i in range(size)])])
    up = [(i, (i + 1) % n) for i in range(n)]
    down = [(i, (i - 1) % n) for i in range(n)]
    pieces = [None] * n
    pieces[0] = x
    fwd = x
    bwd = x
    for s in range(1, (n - 1) // 2 + 1):
        fwd = moved(fwd, axis, up)
        bwd = moved(bwd, axis, down)
        pieces[n - s] = fwd
        pieces[s] = bwd
    if n % 2 == 0:
        h = x.shape[0] // 2
        a = moved(fwd[:h], axis, up)
        b = moved(bwd[h:], axis, down)
        pieces[n // 2] = jnp.concatenate([a, b], 0)
    return jnp.stack(pieces)


def gather_front(block, dims, order):
    held = []
    x = block
    for name in order:
        axis, n, size, me = dims[name]
        x = ring_blocks(x, axis, n, size)
        held.insert(0, name)
    canon = [name for name in ("X", "Y", "Z") if name in dims]
    x = jnp.transpose(x, [held.index(name) for name in canon] + [len(held), len(held) + 1])
    for i, name in enumerate(canon):
        x = jnp.roll(x, dims[name][3], axis=i)
    return x.reshape(-1, x.shape[-1])


def level_dims(level, sizes, idx):
    nxa, nya, ngy = sizes
    xa, ya, gy = idx
    dims = {"Z": ("gy", ngy, ngy, gy)}
    if level == 0:
        dims["Y"] = ("ya", 2, nya, ya % 2)
    else:
        dims["Y"] = ("ya", nya, nya, ya)
    if level == 2:
        dims["X"] = ("xa", 2, nxa, xa % 2)
    elif level == 3:
        dims["X"] = ("xa", nxa, nxa, xa)
    return dims


ORDERS = {
    0: (("Z", "Y"), ("Y", "Z")),
    1: (("Z", "Y"), ("Y", "Z")),
    2: (("Z", "Y", "X"), ("X", "Z", "Y"), ("Y", "X", "Z")),
    3: (("Z", "Y", "X"), ("X", "Z", "Y"), ("Y", "X", "Z")),
}


def split_columns(front, core, groups):
    rows = front.shape[0]
    four = front.reshape(rows, groups, 2, -1)
    mine = lax.dynamic_index_in_dim(four, core, axis=2, keepdims=False).reshape(rows, -1)
    theirs = lax.dynamic_index_in_dim(four, 1 - core, axis=2, keepdims=False).reshape(rows, -1)
    return mine, moved(theirs, "c", [(0, 1), (1, 0)])


def apply_front(front_parts, state, level, sizes, idx):
    own_a, other_a = front_parts
    dims = level_dims(level, sizes, idx)
    orders = ORDERS[level]
    width = state.shape[1]
    count = len(orders)
    edges = [width * i // count // 128 * 128 for i in range(count)] + [width]
    mine = []
    theirs = []
    for i, order in enumerate(orders):
        part = state[:, edges[i] : edges[i + 1]]
        whole = gather_front(part, dims, order)
        mine.append(jnp.dot(own_a, whole, preferred_element_type=jnp.float32))
        theirs.append(jnp.dot(other_a, whole, preferred_element_type=jnp.float32))
    mine = jnp.concatenate(mine, 1)
    theirs = jnp.concatenate(theirs, 1)
    return mine + moved(theirs, "c", [(0, 1), (1, 0)])


def padded_2(cells, sides, width):
    for axis, count, dim in sides:
        ends = count - 1
        head = lax.slice_in_dim(cells, 0, width, axis=dim)
        tail = lax.slice_in_dim(cells, cells.shape[dim] - width, cells.shape[dim], axis=dim)
        cells = jnp.concatenate(
            [
                lax.ppermute(tail, axis, [(i, (i + 1) % count) for i in range(ends)]),
                cells,
                lax.ppermute(head, axis, [((i + 1) % count, i) for i in range(ends)]),
            ],
            axis=dim,
        )
    return cells


def make_local(sizes):
    nxa, nya, ngy = sizes
    ngx = nxa * nya * 2
    leaf_bits = ngx.bit_length() - 4

    def local(
        leaf_load,
        front_zero,
        front_one,
        front_two,
        front_root,
        load_one,
        load_two,
        load_root,
        map_one,
        map_two,
        map_root,
        adjoint,
    ):
        fronts = (front_zero, front_one, front_two, front_root)
        loads = (load_one, load_two, load_root)
        mappings = (map_one, map_two, map_root)
        xa = lax.axis_index("xa")
        ya = lax.axis_index("ya")
        core = lax.axis_index("c")
        row_index = lax.axis_index("gy")
        column = (xa * nya + ya) * 2 + core
        idx = (xa, ya, row_index)
        groups = (1, 1, 2, nxa)
        parts = [
            split_columns(fronts[level], core, groups[level] * (nya if level else 2))
            for level in range(4)
        ]
        state = leaf_load
        for level in range(3):
            bits = leaf_bits + level
            product = apply_front(parts[level], state, level, sizes, idx)
            other = moved(product, GX, [(i, i ^ 1 << bits) for i in range(ngx)])
            upper = column >> bits & 1 == 1
            first = jnp.where(upper, other, product)
            second = jnp.where(upper, product, other)
            half = product.shape[0] // 2
            position = column % 2 ** (bits + 1) * ngy + row_index
            local_map = lax.dynamic_slice_in_dim(mappings[level], position * half, half, 0)
            total = (
                loads[level]
                + jnp.take(first, local_map[:, 0], axis=0)
                + jnp.take(second, local_map[:, 1], axis=0)
            )
            state = total.astype(jnp.bfloat16)
        root_solution = apply_front(parts[3], state, 3, sizes, idx)
        cells_x = adjoint.shape[0]
        cells_y = adjoint.shape[1]
        width = adjoint.shape[2]
        plane = root_solution.reshape(cells_x, cells_y, width)
        stacked = jnp.stack([plane, adjoint])
        padded = padded_2(stacked, ((GX, ngx, 1), ("gy", ngy, 2)), 1)
        padded_u = padded[0]
        padded_a = padded[1]
        gradient = jnp.zeros((cells_x, cells_y, width), jnp.float32)
        for lo_x, lo_y in ((2, 1), (0, 1), (1, 2), (1, 0)):
            near_u = padded_u[lo_x : lo_x + cells_x, lo_y : lo_y + cells_y]
            near_a = padded_a[lo_x : lo_x + cells_x, lo_y : lo_y + cells_y]
            gradient = gradient + (plane - near_u) * (adjoint - near_a)
        return (root_solution, gradient)

    return local


def solution(mesh):
    ngx = mesh.shape["gx"]
    ngy = mesh.shape["gy"]
    nya = 4
    nxa = ngx // (2 * nya)
    devices = np.asarray(mesh.devices).reshape(nxa, nya, 2, ngy)
    fine = Mesh(devices, ALL)
    rows = P(ALL, None)
    in_specs = (rows,) * 8 + (P(), P(), P(), P(GX, "gy", None))
    out_specs = (rows, P(GX, "gy", None))
    return jax.shard_map(
        make_local((nxa, nya, ngy)), mesh=fine, in_specs=in_specs, out_specs=out_specs, check_vma=False
    )
```

```python
import numpy as np
import jax
import jax.numpy as jnp
from jax import lax
from jax.sharding import Mesh, PartitionSpec as P

GX = ("xh", "xl", "yh", "yl", "c")
ALL = GX + ("gy",)
YA = ("yh", "yl")
XA = ("xh", "xl")
GROUP = ("xl", "yl", "c")


def moved(x, axis, pairs):
    return lax.ppermute(x, axis, pairs)


def ring_blocks(x, axis, n, size):
    if n == 2 and size != 2:
        return jnp.stack([x, moved(x, axis, [(i, i ^ 1) for i in range(size)])])
    up = [(i, (i + 1) % n) for i in range(n)]
    down = [(i, (i - 1) % n) for i in range(n)]
    pieces = [None] * n
    pieces[0] = x
    fwd = x
    bwd = x
    for s in range(1, (n - 1) // 2 + 1):
        fwd = moved(fwd, axis, up)
        bwd = moved(bwd, axis, down)
        pieces[n - s] = fwd
        pieces[s] = bwd
    if n % 2 == 0:
        h = x.shape[0] // 2
        a = moved(fwd[:h], axis, up)
        b = moved(bwd[h:], axis, down)
        pieces[n // 2] = jnp.concatenate([a, b], 0)
    return jnp.stack(pieces)


def gather_front(block, dims, order):
    held = []
    x = block
    for name in order:
        axis, n, size, me = dims[name]
        x = ring_blocks(x, axis, n, size)
        held.insert(0, name)
    canon = [name for name in ("X", "Y", "Z") if name in dims]
    x = jnp.transpose(x, [held.index(name) for name in canon] + [len(held), len(held) + 1])
    for i, name in enumerate(canon):
        x = jnp.roll(x, dims[name][3], axis=i)
    return x.reshape(-1, x.shape[-1])


def level_dims(level, sizes, idx):
    nxa, nya, ngy = sizes
    xa, ya, gy = idx
    dims = {"Z": ("gy", ngy, ngy, gy)}
    if level == 0:
        dims["Y"] = (YA, 2, nya, ya % 2)
    else:
        dims["Y"] = (YA, nya, nya, ya)
    if level == 2:
        dims["X"] = (XA, 2, nxa, xa % 2)
    elif level == 3:
        dims["X"] = (XA, nxa, nxa, xa)
    return dims


ORDERS = {
    0: (("Z", "Y"), ("Y", "Z")),
    1: (("Z", "Y"), ("Y", "Z")),
    2: (("Z", "Y", "X"), ("X", "Z", "Y"), ("Y", "X", "Z")),
    3: (("Z", "Y", "X"), ("X", "Z", "Y"), ("Y", "X", "Z")),
}


def split_columns(front, core, groups):
    rows = front.shape[0]
    four = front.reshape(rows, groups, 2, -1)
    mine = lax.dynamic_index_in_dim(four, core, axis=2, keepdims=False).reshape(rows, -1)
    theirs = lax.dynamic_index_in_dim(four, 1 - core, axis=2, keepdims=False).reshape(rows, -1)
    return mine, moved(theirs, "c", [(0, 1), (1, 0)])


def apply_front(front_parts, state, level, sizes, idx):
    own_a, other_a = front_parts
    dims = level_dims(level, sizes, idx)
    orders = ORDERS[level]
    width = state.shape[1]
    count = len(orders)
    edges = [width * i // count // 128 * 128 for i in range(count)] + [width]
    mine = []
    theirs = []
    for i, order in enumerate(orders):
        part = state[:, edges[i] : edges[i + 1]]
        whole = gather_front(part, dims, order)
        mine.append(jnp.dot(own_a, whole, preferred_element_type=jnp.float32))
        theirs.append(jnp.dot(other_a, whole, preferred_element_type=jnp.float32))
    mine = jnp.concatenate(mine, 1)
    theirs = jnp.concatenate(theirs, 1)
    return mine + moved(theirs, "c", [(0, 1), (1, 0)])


def pair_swap(x, axis, size, mask):
    return lax.ppermute(x, axis, [(i, i ^ mask) for i in range(size)])


def spread_front(front, kbits, group, coords):
    rows = front.shape[0]
    names = list(kbits)
    a = front.reshape([rows] + [2] * len(names) + [-1])
    lead = 1
    for axis in group:
        me = coords[axis]
        pos = lead + names.index(axis)
        mine = lax.dynamic_index_in_dim(a, me, axis=pos, keepdims=False)
        theirs = lax.dynamic_index_in_dim(a, 1 - me, axis=pos, keepdims=False)
        got = pair_swap(theirs, axis, 2, 1)
        a = jnp.where(me == 0, jnp.stack([mine, got]), jnp.stack([got, mine]))
        names.remove(axis)
        lead += 1
    return a, names, lead


def doubled(z, steps, coords, sizes):
    cur = z
    for axis, mask, _ in steps:
        got = pair_swap(cur, axis, sizes[axis], mask)
        bit = coords[axis] // mask % 2
        cur = jnp.where(bit == 0, jnp.concatenate([cur, got], 0), jnp.concatenate([got, cur], 0))
    return cur


def apply_grouped(spread, state, steps, group, coords, sizes):
    a, names, lead = spread
    order = [names.index(k) for _, _, k in reversed(steps)]
    perm = list(range(lead)) + [lead + i for i in order] + [lead + len(names)]
    matrix = jnp.transpose(a, perm)
    rows = int(np.prod(matrix.shape[:lead]))
    matrix = matrix.reshape(rows, -1)
    whole = doubled(state, steps, coords, sizes)
    p = jnp.dot(matrix, whole, preferred_element_type=jnp.float32)
    for axis in reversed(group):
        p = p.reshape(2, -1, p.shape[-1])
        me = coords[axis]
        mine = lax.dynamic_index_in_dim(p, me, axis=0, keepdims=False)
        theirs = lax.dynamic_index_in_dim(p, 1 - me, axis=0, keepdims=False)
        p = mine + pair_swap(theirs, axis, 2, 1)
    return p


def padded_2(cells, sides, width):
    for axis, count, dim in sides:
        ends = count - 1
        head = lax.slice_in_dim(cells, 0, width, axis=dim)
        tail = lax.slice_in_dim(cells, cells.shape[dim] - width, cells.shape[dim], axis=dim)
        cells = jnp.concatenate(
            [
                lax.ppermute(tail, axis, [(i, (i + 1) % count) for i in range(ends)]),
                cells,
                lax.ppermute(head, axis, [((i + 1) % count, i) for i in range(ends)]),
            ],
            axis=dim,
        )
    return cells


def make_local(sizes):
    nxa, nya, ngy = sizes
    ngx = nxa * nya * 2
    leaf_bits = ngx.bit_length() - 4

    def local(
        leaf_load,
        front_zero,
        front_one,
        front_two,
        front_root,
        load_one,
        load_two,
        load_root,
        map_one,
        map_two,
        map_root,
        adjoint,
    ):
        fronts = (front_zero, front_one, front_two, front_root)
        loads = (load_one, load_two, load_root)
        mappings = (map_one, map_two, map_root)
        coords = {name: lax.axis_index(name) for name in ALL}
        xa = coords["xh"] * 2 + coords["xl"]
        ya = coords["yh"] * 2 + coords["yl"]
        core = coords["c"]
        row_index = coords["gy"]
        column = (xa * nya + ya) * 2 + core
        idx = (xa, ya, row_index)
        axis_sizes = {name: 2 for name in GX}
        axis_sizes["gy"] = ngy
        gy_bits = [("g%d" % b, 1 << b) for b in reversed(range(ngy.bit_length() - 1))]
        kbits = {
            2: ["xl", "yh", "yl", "c"] + [name for name, _ in gy_bits],
            3: ["xh", "xl", "yh", "yl", "c"] + [name for name, _ in gy_bits],
        }
        high = [("gy",) + tuple(reversed(gy_bits[0]))]
        low = [("gy",) + tuple(reversed(bit)) for bit in gy_bits[1:]]
        steps = {
            2: high + [("yh", 1, "yh")] + low,
            3: high + [("xh", 1, "xh"), ("yh", 1, "yh")] + low,
        }
        parts = [split_columns(fronts[level], core, (2, nya)[level]) for level in range(2)]
        parts += [spread_front(fronts[level], kbits[level], GROUP, coords) for level in (2, 3)]

        def product_of(level, state):
            if level < 2:
                return apply_front(parts[level], state, level, sizes, idx)
            return apply_grouped(parts[level], state, steps[level], GROUP, coords, axis_sizes)

        state = leaf_load
        for level in range(3):
            bits = leaf_bits + level
            product = product_of(level, state)
            other = moved(product, GX, [(i, i ^ 1 << bits) for i in range(ngx)])
            upper = column >> bits & 1 == 1
            first = jnp.where(upper, other, product)
            second = jnp.where(upper, product, other)
            half = product.shape[0] // 2
            position = column % 2 ** (bits + 1) * ngy + row_index
            local_map = lax.dynamic_slice_in_dim(mappings[level], position * half, half, 0)
            total = (
                loads[level]
                + jnp.take(first, local_map[:, 0], axis=0)
                + jnp.take(second, local_map[:, 1], axis=0)
            )
            state = total.astype(jnp.bfloat16)
        root_solution = product_of(3, state)
        cells_x = adjoint.shape[0]
        cells_y = adjoint.shape[1]
        width = adjoint.shape[2]
        plane = root_solution.reshape(cells_x, cells_y, width)
        stacked = jnp.stack([plane, adjoint])
        padded = padded_2(stacked, ((GX, ngx, 1), ("gy", ngy, 2)), 1)
        padded_u = padded[0]
        padded_a = padded[1]
        gradient = jnp.zeros((cells_x, cells_y, width), jnp.float32)
        for lo_x, lo_y in ((2, 1), (0, 1), (1, 2), (1, 0)):
            near_u = padded_u[lo_x : lo_x + cells_x, lo_y : lo_y + cells_y]
            near_a = padded_a[lo_x : lo_x + cells_x, lo_y : lo_y + cells_y]
            gradient = gradient + (plane - near_u) * (adjoint - near_a)
        return (root_solution, gradient)

    return local


def solution(mesh):
    ngx = mesh.shape["gx"]
    ngy = mesh.shape["gy"]
    nya = 4
    nxa = ngx // (2 * nya)
    devices = np.asarray(mesh.devices).reshape(2, nxa // 2, 2, nya // 2, 2, ngy)
    fine = Mesh(devices, ALL)
    rows = P(ALL, None)
    in_specs = (rows,) * 8 + (P(), P(), P(), P(GX, "gy", None))
    out_specs = (rows, P(GX, "gy", None))
    return jax.shard_map(
        make_local((nxa, nya, ngy)), mesh=fine, in_specs=in_specs, out_specs=out_specs, check_vma=False
    )
```

```python
import numpy as np
import jax
import jax.numpy as jnp
from jax import lax
from jax.sharding import Mesh, PartitionSpec as P

GX = ("xh", "xl", "yh", "yl", "c")
ALL = GX + ("gy",)
YA = ("yh", "yl")
XA = ("xh", "xl")
GROUP = ("xl", "yl", "c")


def moved(x, axis, pairs):
    return lax.ppermute(x, axis, pairs)


def ring_blocks(x, axis, n, size):
    if n == 2 and size != 2:
        got = moved(x, axis, [(i, i ^ 1) for i in range(size)])
        return jnp.stack([x, got]), got
    up = [(i, (i + 1) % n) for i in range(n)]
    down = [(i, (i - 1) % n) for i in range(n)]
    pieces = [None] * n
    pieces[0] = x
    fwd = x
    bwd = x
    for s in range(1, (n - 1) // 2 + 1):
        fwd = moved(fwd, axis, up)
        bwd = moved(bwd, axis, down)
        pieces[n - s] = fwd
        pieces[s] = bwd
    if n % 2 == 0:
        h = x.shape[0] // 2
        a = moved(fwd[:h], axis, up)
        b = moved(bwd[h:], axis, down)
        pieces[n // 2] = jnp.concatenate([a, b], 0)
    return jnp.stack(pieces), pieces[1]


def gather_front(block, dims, order):
    held = []
    x = block
    anchor = None
    for name in order:
        axis, n, size, me = dims[name]
        x, got = ring_blocks(x, axis, n, size)
        anchor = got if anchor is None else anchor
        held.insert(0, name)
    canon = [name for name in ("X", "Y", "Z") if name in dims]
    x = jnp.transpose(x, [held.index(name) for name in canon] + [len(held), len(held) + 1])
    for i, name in enumerate(canon):
        x = jnp.roll(x, dims[name][3], axis=i)
    return x.reshape(-1, x.shape[-1]), anchor


def level_dims(level, sizes, idx):
    nxa, nya, ngy = sizes
    xa, ya, gy = idx
    dims = {"Z": ("gy", ngy, ngy, gy)}
    if level == 0:
        dims["Y"] = (YA, 2, nya, ya % 2)
    else:
        dims["Y"] = (YA, nya, nya, ya)
    if level == 2:
        dims["X"] = (XA, 2, nxa, xa % 2)
    elif level == 3:
        dims["X"] = (XA, nxa, nxa, xa)
    return dims


ORDERS = {
    0: (("Y", "Z"),),
    1: (("Y", "Z"),),
    2: (("Z", "Y", "X"), ("X", "Z", "Y"), ("Y", "X", "Z")),
    3: (("Z", "Y", "X"), ("X", "Z", "Y"), ("Y", "X", "Z")),
}


def split_columns(front, core, groups):
    rows = front.shape[0]
    four = front.reshape(rows, groups, 2, -1)
    mine = lax.dynamic_index_in_dim(four, core, axis=2, keepdims=False).reshape(rows, -1)
    theirs = lax.dynamic_index_in_dim(four, 1 - core, axis=2, keepdims=False).reshape(rows, -1)
    return mine, moved(theirs, "c", [(0, 1), (1, 0)])


def apply_front(prepare, state, level, sizes, idx):
    dims = level_dims(level, sizes, idx)
    orders = ORDERS[level]
    width = state.shape[1]
    count = len(orders)
    edges = [width * i // count // 128 * 128 for i in range(count)] + [width]
    mine = []
    theirs = []
    wholes = []
    anchor = None
    for i, order in enumerate(orders):
        part = state[:, edges[i] : edges[i + 1]]
        whole, got = gather_front(part, dims, order)
        wholes.append(whole)
        anchor = got if anchor is None else anchor
    own_a, other_a = prepare(anchor)
    for whole in wholes:
        mine.append(jnp.dot(own_a, whole, preferred_element_type=jnp.float32))
        theirs.append(jnp.dot(other_a, whole, preferred_element_type=jnp.float32))
    mine = jnp.concatenate(mine, 1)
    theirs = jnp.concatenate(theirs, 1)
    return mine + moved(theirs, "c", [(0, 1), (1, 0)])


def pair_swap(x, axis, size, mask):
    return lax.ppermute(x, axis, [(i, i ^ mask) for i in range(size)])


def spread_front(front, kbits, group, coords):
    rows = front.shape[0]
    names = list(kbits)
    a = front.reshape([rows] + [2] * len(names) + [-1])
    lead = 1
    for axis in group:
        me = coords[axis]
        pos = lead + names.index(axis)
        mine = lax.dynamic_index_in_dim(a, me, axis=pos, keepdims=False)
        theirs = lax.dynamic_index_in_dim(a, 1 - me, axis=pos, keepdims=False)
        got = pair_swap(theirs, axis, 2, 1)
        a = jnp.where(me == 0, jnp.stack([mine, got]), jnp.stack([got, mine]))
        names.remove(axis)
        lead += 1
    return a, names, lead


def doubled(z, steps, coords, sizes):
    cur = z
    for axis, mask, _ in steps:
        got = pair_swap(cur, axis, sizes[axis], mask)
        bit = coords[axis] // mask % 2
        cur = jnp.where(bit == 0, jnp.concatenate([cur, got], 0), jnp.concatenate([got, cur], 0))
    return cur


def apply_grouped(spread, state, steps, group, coords, sizes):
    a, names, lead = spread
    order = [names.index(k) for _, _, k in reversed(steps)]
    perm = list(range(lead)) + [lead + i for i in order] + [lead + len(names)]
    matrix = jnp.transpose(a, perm)
    rows = int(np.prod(matrix.shape[:lead]))
    matrix = matrix.reshape(rows, -1)
    whole = doubled(state, steps, coords, sizes)
    p = jnp.dot(matrix, whole, preferred_element_type=jnp.float32)
    for axis in reversed(group):
        p = p.reshape(2, -1, p.shape[-1])
        me = coords[axis]
        mine = lax.dynamic_index_in_dim(p, me, axis=0, keepdims=False)
        theirs = lax.dynamic_index_in_dim(p, 1 - me, axis=0, keepdims=False)
        p = mine + pair_swap(theirs, axis, 2, 1)
    return p


def padded_2(cells, sides, width):
    for axis, count, dim in sides:
        ends = count - 1
        head = lax.slice_in_dim(cells, 0, width, axis=dim)
        tail = lax.slice_in_dim(cells, cells.shape[dim] - width, cells.shape[dim], axis=dim)
        cells = jnp.concatenate(
            [
                lax.ppermute(tail, axis, [(i, (i + 1) % count) for i in range(ends)]),
                cells,
                lax.ppermute(head, axis, [((i + 1) % count, i) for i in range(ends)]),
            ],
            axis=dim,
        )
    return cells


def make_local(sizes):
    nxa, nya, ngy = sizes
    ngx = nxa * nya * 2
    leaf_bits = ngx.bit_length() - 4

    def local(
        leaf_load,
        front_zero,
        front_one,
        front_two,
        front_root,
        load_one,
        load_two,
        load_root,
        map_one,
        map_two,
        map_root,
        adjoint,
    ):
        fronts = (front_zero, front_one, front_two, front_root)
        loads = (load_one, load_two, load_root)
        mappings = (map_one, map_two, map_root)
        coords = {name: lax.axis_index(name) for name in ALL}
        xa = coords["xh"] * 2 + coords["xl"]
        ya = coords["yh"] * 2 + coords["yl"]
        core = coords["c"]
        row_index = coords["gy"]
        column = (xa * nya + ya) * 2 + core
        idx = (xa, ya, row_index)
        axis_sizes = {name: 2 for name in GX}
        axis_sizes["gy"] = ngy
        gy_bits = [("g%d" % b, 1 << b) for b in reversed(range(ngy.bit_length() - 1))]
        kbits = {
            2: ["xl", "yh", "yl", "c"] + [name for name, _ in gy_bits],
            3: ["xh", "xl", "yh", "yl", "c"] + [name for name, _ in gy_bits],
        }
        high = [("gy",) + tuple(reversed(gy_bits[0]))]
        low = [("gy",) + tuple(reversed(bit)) for bit in gy_bits[1:]]
        steps = {
            2: high + [("yh", 1, "yh")] + low,
            3: high + [("xh", 1, "xh"), ("yh", 1, "yh")] + low,
        }
        parts = {}

        def prepare(anchor):
            tied = lax.optimization_barrier((fronts, anchor))[0]
            parts[1] = split_columns(tied[1], core, nya)
            for level in (2, 3):
                parts[level] = spread_front(tied[level], kbits[level], GROUP, coords)
            return split_columns(tied[0], core, 2)

        def product_of(level, state):
            if level == 0:
                return apply_front(prepare, state, level, sizes, idx)
            if level == 1:
                return apply_front(lambda anchor: parts[1], state, level, sizes, idx)
            return apply_grouped(parts[level], state, steps[level], GROUP, coords, axis_sizes)

        state = leaf_load
        for level in range(3):
            bits = leaf_bits + level
            if level == 1:
                held = (parts[1], parts[2][0], parts[3][0])
                state, held = lax.optimization_barrier((state, held))
                parts[1] = held[0]
                parts[2] = (held[1],) + parts[2][1:]
                parts[3] = (held[2],) + parts[3][1:]
            product = product_of(level, state)
            other = moved(product, GX, [(i, i ^ 1 << bits) for i in range(ngx)])
            upper = column >> bits & 1 == 1
            first = jnp.where(upper, other, product)
            second = jnp.where(upper, product, other)
            half = product.shape[0] // 2
            position = column % 2 ** (bits + 1) * ngy + row_index
            local_map = lax.dynamic_slice_in_dim(mappings[level], position * half, half, 0)
            total = (
                loads[level]
                + jnp.take(first, local_map[:, 0], axis=0)
                + jnp.take(second, local_map[:, 1], axis=0)
            )
            state = total.astype(jnp.bfloat16)
        root_solution = product_of(3, state)
        cells_x = adjoint.shape[0]
        cells_y = adjoint.shape[1]
        width = adjoint.shape[2]
        plane = root_solution.reshape(cells_x, cells_y, width)
        stacked = jnp.stack([plane, adjoint])
        padded = padded_2(stacked, ((GX, ngx, 1), ("gy", ngy, 2)), 1)
        padded_u = padded[0]
        padded_a = padded[1]
        gradient = jnp.zeros((cells_x, cells_y, width), jnp.float32)
        for lo_x, lo_y in ((2, 1), (0, 1), (1, 2), (1, 0)):
            near_u = padded_u[lo_x : lo_x + cells_x, lo_y : lo_y + cells_y]
            near_a = padded_a[lo_x : lo_x + cells_x, lo_y : lo_y + cells_y]
            gradient = gradient + (plane - near_u) * (adjoint - near_a)
        return (root_solution, gradient)

    return local


def solution(mesh):
    ngx = mesh.shape["gx"]
    ngy = mesh.shape["gy"]
    nya = 4
    nxa = ngx // (2 * nya)
    devices = np.asarray(mesh.devices).reshape(2, nxa // 2, 2, nya // 2, 2, ngy)
    fine = Mesh(devices, ALL)
    rows = P(ALL, None)
    in_specs = (rows,) * 8 + (P(), P(), P(), P(GX, "gy", None))
    out_specs = (rows, P(GX, "gy", None))
    return jax.shard_map(
        make_local((nxa, nya, ngy)), mesh=fine, in_specs=in_specs, out_specs=out_specs, check_vma=False
    )
```

```python
import numpy as np
import jax
import jax.numpy as jnp
from jax import lax
from jax.sharding import Mesh, PartitionSpec as P

GX = ("xh", "xl", "yh", "yl", "c")
ALL = GX + ("gy",)
YA = ("yh", "yl")
XA = ("xh", "xl")
GROUP = ("xl", "yl", "c")


def moved(x, axis, pairs):
    return lax.ppermute(x, axis, pairs)


def ring_blocks(x, axis, n, size):
    if n == 2 and size != 2:
        got = moved(x, axis, [(i, i ^ 1) for i in range(size)])
        return jnp.stack([x, got]), got
    up = [(i, (i + 1) % n) for i in range(n)]
    down = [(i, (i - 1) % n) for i in range(n)]
    pieces = [None] * n
    pieces[0] = x
    fwd = x
    bwd = x
    for s in range(1, (n - 1) // 2 + 1):
        fwd = moved(fwd, axis, up)
        bwd = moved(bwd, axis, down)
        pieces[n - s] = fwd
        pieces[s] = bwd
    if n % 2 == 0:
        h = x.shape[0] // 2
        a = moved(fwd[:h], axis, up)
        b = moved(bwd[h:], axis, down)
        pieces[n // 2] = jnp.concatenate([a, b], 0)
    return jnp.stack(pieces), pieces[1]


def gather_front(block, dims, order):
    held = []
    x = block
    anchor = None
    for name in order:
        axis, n, size, me = dims[name]
        x, got = ring_blocks(x, axis, n, size)
        anchor = got if anchor is None else anchor
        held.insert(0, name)
    canon = [name for name in ("X", "Y", "Z") if name in dims]
    x = jnp.transpose(x, [held.index(name) for name in canon] + [len(held), len(held) + 1])
    for i, name in enumerate(canon):
        x = jnp.roll(x, dims[name][3], axis=i)
    return x.reshape(-1, x.shape[-1]), anchor


def level_dims(level, sizes, idx):
    nxa, nya, ngy = sizes
    xa, ya, gy = idx
    dims = {"Z": ("gy", ngy, ngy, gy)}
    if level == 0:
        dims["Y"] = (YA, 2, nya, ya % 2)
    else:
        dims["Y"] = (YA, nya, nya, ya)
    if level == 2:
        dims["X"] = (XA, 2, nxa, xa % 2)
    elif level == 3:
        dims["X"] = (XA, nxa, nxa, xa)
    return dims


ORDERS = {
    0: (("Z", "Y"), ("Y", "Z")),
    1: (("Y", "Z"),),
    2: (("Z", "Y", "X"), ("X", "Z", "Y"), ("Y", "X", "Z")),
    3: (("Z", "Y", "X"), ("X", "Z", "Y"), ("Y", "X", "Z")),
}


def split_columns(front, core, groups):
    rows = front.shape[0]
    four = front.reshape(rows, groups, 2, -1)
    mine = lax.dynamic_index_in_dim(four, core, axis=2, keepdims=False).reshape(rows, -1)
    theirs = lax.dynamic_index_in_dim(four, 1 - core, axis=2, keepdims=False).reshape(rows, -1)
    return mine, moved(theirs, "c", [(0, 1), (1, 0)])


def apply_front(prepare, state, level, sizes, idx):
    dims = level_dims(level, sizes, idx)
    orders = ORDERS[level]
    width = state.shape[1]
    count = len(orders)
    edges = [width * i // count // 128 * 128 for i in range(count)] + [width]
    mine = []
    theirs = []
    wholes = []
    anchor = None
    for i, order in enumerate(orders):
        part = state[:, edges[i] : edges[i + 1]]
        whole, got = gather_front(part, dims, order)
        wholes.append(whole)
        anchor = got if anchor is None else anchor
    own_a, other_a = prepare(anchor)
    for whole in wholes:
        mine.append(jnp.dot(own_a, whole, preferred_element_type=jnp.float32))
        theirs.append(jnp.dot(other_a, whole, preferred_element_type=jnp.float32))
    mine = jnp.concatenate(mine, 1)
    theirs = jnp.concatenate(theirs, 1)
    return mine + moved(theirs, "c", [(0, 1), (1, 0)])


def pair_swap(x, axis, size, mask):
    return lax.ppermute(x, axis, [(i, i ^ mask) for i in range(size)])


def spread_front(front, kbits, group, coords):
    rows = front.shape[0]
    names = list(kbits)
    a = front.reshape([rows] + [2] * len(names) + [-1])
    lead = 1
    for axis in group:
        me = coords[axis]
        pos = lead + names.index(axis)
        mine = lax.dynamic_index_in_dim(a, me, axis=pos, keepdims=False)
        theirs = lax.dynamic_index_in_dim(a, 1 - me, axis=pos, keepdims=False)
        got = pair_swap(theirs, axis, 2, 1)
        a = jnp.where(me == 0, jnp.stack([mine, got]), jnp.stack([got, mine]))
        names.remove(axis)
        lead += 1
    return a, names, lead


def doubled(z, steps, coords, sizes):
    cur = z
    for axis, mask, _ in steps:
        got = pair_swap(cur, axis, sizes[axis], mask)
        bit = coords[axis] // mask % 2
        cur = jnp.where(bit == 0, jnp.concatenate([cur, got], 0), jnp.concatenate([got, cur], 0))
    return cur


def apply_grouped(spread, state, steps, group, coords, sizes):
    a, names, lead = spread
    order = [names.index(k) for _, _, k in reversed(steps)]
    perm = list(range(lead)) + [lead + i for i in order] + [lead + len(names)]
    matrix = jnp.transpose(a, perm)
    rows = int(np.prod(matrix.shape[:lead]))
    matrix = matrix.reshape(rows, -1)
    whole = doubled(state, steps, coords, sizes)
    p = jnp.dot(matrix, whole, preferred_element_type=jnp.float32)
    for axis in reversed(group):
        p = p.reshape(2, -1, p.shape[-1])
        me = coords[axis]
        mine = lax.dynamic_index_in_dim(p, me, axis=0, keepdims=False)
        theirs = lax.dynamic_index_in_dim(p, 1 - me, axis=0, keepdims=False)
        p = mine + pair_swap(theirs, axis, 2, 1)
    return p


def padded_2(cells, sides, width):
    for axis, count, dim in sides:
        ends = count - 1
        head = lax.slice_in_dim(cells, 0, width, axis=dim)
        tail = lax.slice_in_dim(cells, cells.shape[dim] - width, cells.shape[dim], axis=dim)
        cells = jnp.concatenate(
            [
                lax.ppermute(tail, axis, [(i, (i + 1) % count) for i in range(ends)]),
                cells,
                lax.ppermute(head, axis, [((i + 1) % count, i) for i in range(ends)]),
            ],
            axis=dim,
        )
    return cells


def make_local(sizes):
    nxa, nya, ngy = sizes
    ngx = nxa * nya * 2
    leaf_bits = ngx.bit_length() - 4

    def local(
        leaf_load,
        front_zero,
        front_one,
        front_two,
        front_root,
        load_one,
        load_two,
        load_root,
        map_one,
        map_two,
        map_root,
        adjoint,
    ):
        fronts = (front_zero, front_one, front_two, front_root)
        loads = (load_one, load_two, load_root)
        mappings = (map_one, map_two, map_root)
        coords = {name: lax.axis_index(name) for name in ALL}
        xa = coords["xh"] * 2 + coords["xl"]
        ya = coords["yh"] * 2 + coords["yl"]
        core = coords["c"]
        row_index = coords["gy"]
        column = (xa * nya + ya) * 2 + core
        idx = (xa, ya, row_index)
        axis_sizes = {name: 2 for name in GX}
        axis_sizes["gy"] = ngy
        gy_bits = [("g%d" % b, 1 << b) for b in reversed(range(ngy.bit_length() - 1))]
        kbits = {
            2: ["xl", "yh", "yl", "c"] + [name for name, _ in gy_bits],
            3: ["xh", "xl", "yh", "yl", "c"] + [name for name, _ in gy_bits],
        }
        high = [("gy",) + tuple(reversed(gy_bits[0]))]
        low = [("gy",) + tuple(reversed(bit)) for bit in gy_bits[1:]]
        steps = {
            2: high + [("yh", 1, "yh")] + low,
            3: high + [("xh", 1, "xh"), ("yh", 1, "yh")] + low,
        }
        parts = {}

        def prepare(anchor):
            tied = lax.optimization_barrier((fronts, anchor))[0]
            parts[1] = split_columns(tied[1], core, nya)
            for level in (2, 3):
                parts[level] = spread_front(tied[level], kbits[level], GROUP, coords)
            return split_columns(tied[0], core, 2)

        def product_of(level, state):
            if level == 0:
                return apply_front(prepare, state, level, sizes, idx)
            if level == 1:
                return apply_front(lambda anchor: parts[1], state, level, sizes, idx)
            return apply_grouped(parts[level], state, steps[level], GROUP, coords, axis_sizes)

        state = leaf_load
        for level in range(3):
            bits = leaf_bits + level
            if level == 1:
                held = (parts[1], parts[2][0], parts[3][0])
                state, held = lax.optimization_barrier((state, held))
                parts[1] = held[0]
                parts[2] = (held[1],) + parts[2][1:]
                parts[3] = (held[2],) + parts[3][1:]
            product = product_of(level, state)
            other = moved(product, GX, [(i, i ^ 1 << bits) for i in range(ngx)])
            upper = column >> bits & 1 == 1
            first = jnp.where(upper, other, product)
            second = jnp.where(upper, product, other)
            half = product.shape[0] // 2
            position = column % 2 ** (bits + 1) * ngy + row_index
            local_map = lax.dynamic_slice_in_dim(mappings[level], position * half, half, 0)
            total = (
                loads[level]
                + jnp.take(first, local_map[:, 0], axis=0)
                + jnp.take(second, local_map[:, 1], axis=0)
            )
            state = total.astype(jnp.bfloat16)
        root_solution = product_of(3, state)
        cells_x = adjoint.shape[0]
        cells_y = adjoint.shape[1]
        width = adjoint.shape[2]
        plane = root_solution.reshape(cells_x, cells_y, width)
        stacked = jnp.stack([plane, adjoint])
        padded = padded_2(stacked, ((GX, ngx, 1), ("gy", ngy, 2)), 1)
        padded_u = padded[0]
        padded_a = padded[1]
        gradient = jnp.zeros((cells_x, cells_y, width), jnp.float32)
        for lo_x, lo_y in ((2, 1), (0, 1), (1, 2), (1, 0)):
            near_u = padded_u[lo_x : lo_x + cells_x, lo_y : lo_y + cells_y]
            near_a = padded_a[lo_x : lo_x + cells_x, lo_y : lo_y + cells_y]
            gradient = gradient + (plane - near_u) * (adjoint - near_a)
        return (root_solution, gradient)

    return local


def solution(mesh):
    ngx = mesh.shape["gx"]
    ngy = mesh.shape["gy"]
    nya = 4
    nxa = ngx // (2 * nya)
    devices = np.asarray(mesh.devices).reshape(2, nxa // 2, 2, nya // 2, 2, ngy)
    fine = Mesh(devices, ALL)
    rows = P(ALL, None)
    in_specs = (rows,) * 8 + (P(), P(), P(), P(GX, "gy", None))
    out_specs = (rows, P(GX, "gy", None))
    return jax.shard_map(
        make_local((nxa, nya, ngy)), mesh=fine, in_specs=in_specs, out_specs=out_specs, check_vma=False
    )
```

```python
import numpy as np
import jax
import jax.numpy as jnp
from jax import lax
from jax.sharding import Mesh, PartitionSpec as P

GX = ("xh", "xl", "yh", "yl", "c")
ALL = GX + ("gy",)
YA = ("yh", "yl")
XA = ("xh", "xl")
GROUPS = {2: ("xl", "c"), 3: ("xh", "xl", "c")}


def moved(x, axis, pairs):
    return lax.ppermute(x, axis, pairs)


def ring_blocks(x, axis, n, size):
    if n == 2 and size != 2:
        got = moved(x, axis, [(i, i ^ 1) for i in range(size)])
        return jnp.stack([x, got]), got
    up = [(i, (i + 1) % n) for i in range(n)]
    down = [(i, (i - 1) % n) for i in range(n)]
    pieces = [None] * n
    pieces[0] = x
    fwd = x
    bwd = x
    for s in range(1, (n - 1) // 2 + 1):
        fwd = moved(fwd, axis, up)
        bwd = moved(bwd, axis, down)
        pieces[n - s] = fwd
        pieces[s] = bwd
    if n % 2 == 0:
        h = x.shape[0] // 2
        a = moved(fwd[:h], axis, up)
        b = moved(bwd[h:], axis, down)
        pieces[n // 2] = jnp.concatenate([a, b], 0)
    return jnp.stack(pieces), pieces[1]


def gather_front(block, dims, order):
    held = []
    x = block
    anchor = None
    for name in order:
        axis, n, size, me = dims[name]
        x, got = ring_blocks(x, axis, n, size)
        anchor = got if anchor is None else anchor
        held.insert(0, name)
    canon = [name for name in ("X", "Y", "Z") if name in dims]
    x = jnp.transpose(x, [held.index(name) for name in canon] + [len(held), len(held) + 1])
    for i, name in enumerate(canon):
        x = jnp.roll(x, dims[name][3], axis=i)
    return x.reshape(-1, x.shape[-1]), anchor


def level_dims(level, sizes, idx):
    nxa, nya, ngy = sizes
    xa, ya, gy = idx
    dims = {"Z": ("gy", ngy, ngy, gy)}
    if level == 0:
        dims["Y"] = (YA, 2, nya, ya % 2)
    else:
        dims["Y"] = (YA, nya, nya, ya)
    if level == 2:
        dims["X"] = (XA, 2, nxa, xa % 2)
    elif level == 3:
        dims["X"] = (XA, nxa, nxa, xa)
    return dims


ORDERS = {
    0: (("Y", "Z"),),
    1: (("Y", "Z"),),
    2: (("Z", "Y", "X"), ("X", "Z", "Y"), ("Y", "X", "Z")),
    3: (("Z", "Y", "X"), ("X", "Z", "Y"), ("Y", "X", "Z")),
}


def split_columns(front, core, groups):
    rows = front.shape[0]
    four = front.reshape(rows, groups, 2, -1)
    mine = lax.dynamic_index_in_dim(four, core, axis=2, keepdims=False).reshape(rows, -1)
    theirs = lax.dynamic_index_in_dim(four, 1 - core, axis=2, keepdims=False).reshape(rows, -1)
    return mine, moved(theirs, "c", [(0, 1), (1, 0)])


def apply_front(prepare, state, level, sizes, idx):
    dims = level_dims(level, sizes, idx)
    orders = ORDERS[level]
    width = state.shape[1]
    count = len(orders)
    edges = [width * i // count // 128 * 128 for i in range(count)] + [width]
    mine = []
    theirs = []
    wholes = []
    anchor = None
    for i, order in enumerate(orders):
        part = state[:, edges[i] : edges[i + 1]]
        whole, got = gather_front(part, dims, order)
        wholes.append(whole)
        anchor = got if anchor is None else anchor
    own_a, other_a = prepare(anchor)
    for whole in wholes:
        mine.append(jnp.dot(own_a, whole, preferred_element_type=jnp.float32))
        theirs.append(jnp.dot(other_a, whole, preferred_element_type=jnp.float32))
    mine = jnp.concatenate(mine, 1)
    theirs = jnp.concatenate(theirs, 1)
    return mine + moved(theirs, "c", [(0, 1), (1, 0)])


def pair_swap(x, axis, size, mask):
    return lax.ppermute(x, axis, [(i, i ^ mask) for i in range(size)])


def spread_front(front, kbits, group, coords):
    rows = front.shape[0]
    names = list(kbits)
    a = front.reshape([rows] + [2] * len(names) + [-1])
    lead = 1
    for axis in group:
        me = coords[axis]
        pos = lead + names.index(axis)
        mine = lax.dynamic_index_in_dim(a, me, axis=pos, keepdims=False)
        theirs = lax.dynamic_index_in_dim(a, 1 - me, axis=pos, keepdims=False)
        got = pair_swap(theirs, axis, 2, 1)
        a = jnp.where(me == 0, jnp.stack([mine, got]), jnp.stack([got, mine]))
        names.remove(axis)
        lead += 1
    return a, names, lead


def doubled(z, steps, coords, sizes):
    cur = z
    for axis, mask, _ in steps:
        got = pair_swap(cur, axis, sizes[axis], mask)
        bit = coords[axis] // mask % 2
        cur = jnp.where(bit == 0, jnp.concatenate([cur, got], 0), jnp.concatenate([got, cur], 0))
    return cur


def apply_grouped(spread, state, steps, group, coords, sizes):
    a, names, lead = spread
    order = [names.index(k) for _, _, k in reversed(steps)]
    perm = list(range(lead)) + [lead + i for i in order] + [lead + len(names)]
    matrix = jnp.transpose(a, perm)
    rows = int(np.prod(matrix.shape[:lead]))
    matrix = matrix.reshape(rows, -1)
    whole = doubled(state, steps, coords, sizes)
    p = jnp.dot(matrix, whole, preferred_element_type=jnp.float32)
    for axis in reversed(group):
        p = p.reshape(2, -1, p.shape[-1])
        me = coords[axis]
        mine = lax.dynamic_index_in_dim(p, me, axis=0, keepdims=False)
        theirs = lax.dynamic_index_in_dim(p, 1 - me, axis=0, keepdims=False)
        p = mine + pair_swap(theirs, axis, 2, 1)
    return p


def padded_2(cells, sides, width):
    for axis, count, dim in sides:
        ends = count - 1
        head = lax.slice_in_dim(cells, 0, width, axis=dim)
        tail = lax.slice_in_dim(cells, cells.shape[dim] - width, cells.shape[dim], axis=dim)
        cells = jnp.concatenate(
            [
                lax.ppermute(tail, axis, [(i, (i + 1) % count) for i in range(ends)]),
                cells,
                lax.ppermute(head, axis, [((i + 1) % count, i) for i in range(ends)]),
            ],
            axis=dim,
        )
    return cells


def make_local(sizes):
    nxa, nya, ngy = sizes
    ngx = nxa * nya * 2
    leaf_bits = ngx.bit_length() - 4

    def local(
        leaf_load,
        front_zero,
        front_one,
        front_two,
        front_root,
        load_one,
        load_two,
        load_root,
        map_one,
        map_two,
        map_root,
        adjoint,
    ):
        fronts = (front_zero, front_one, front_two, front_root)
        loads = (load_one, load_two, load_root)
        mappings = (map_one, map_two, map_root)
        coords = {name: lax.axis_index(name) for name in ALL}
        xa = coords["xh"] * 2 + coords["xl"]
        ya = coords["yh"] * 2 + coords["yl"]
        core = coords["c"]
        row_index = coords["gy"]
        column = (xa * nya + ya) * 2 + core
        idx = (xa, ya, row_index)
        axis_sizes = {name: 2 for name in GX}
        axis_sizes["gy"] = ngy
        gy_bits = [("g%d" % b, 1 << b) for b in reversed(range(ngy.bit_length() - 1))]
        kbits = {
            2: ["xl", "yh", "yl", "c"] + [name for name, _ in gy_bits],
            3: ["xh", "xl", "yh", "yl", "c"] + [name for name, _ in gy_bits],
        }
        high = [("gy",) + tuple(reversed(gy_bits[0]))]
        low = [("gy",) + tuple(reversed(bit)) for bit in gy_bits[1:]]
        steps = {
            2: high + [("yh", 1, "yh"), ("yl", 1, "yl")] + low,
            3: high + [("yh", 1, "yh"), ("yl", 1, "yl")] + low,
        }
        parts = {}

        def prepare(anchor):
            tied = lax.optimization_barrier((fronts, anchor))[0]
            parts[1] = split_columns(tied[1], core, nya)
            for level in (2, 3):
                parts[level] = spread_front(tied[level], kbits[level], GROUPS[level], coords)
            return split_columns(tied[0], core, 2)

        def product_of(level, state):
            if level == 0:
                return apply_front(prepare, state, level, sizes, idx)
            if level == 1:
                return apply_front(lambda anchor: parts[1], state, level, sizes, idx)
            return apply_grouped(parts[level], state, steps[level], GROUPS[level], coords, axis_sizes)

        state = leaf_load
        for level in range(3):
            bits = leaf_bits + level
            if level == 1:
                held = (parts[1], parts[2][0], parts[3][0])
                state, held = lax.optimization_barrier((state, held))
                parts[1] = held[0]
                parts[2] = (held[1],) + parts[2][1:]
                parts[3] = (held[2],) + parts[3][1:]
            product = product_of(level, state)
            other = moved(product, GX, [(i, i ^ 1 << bits) for i in range(ngx)])
            upper = column >> bits & 1 == 1
            first = jnp.where(upper, other, product)
            second = jnp.where(upper, product, other)
            half = product.shape[0] // 2
            position = column % 2 ** (bits + 1) * ngy + row_index
            local_map = lax.dynamic_slice_in_dim(mappings[level], position * half, half, 0)
            total = (
                loads[level]
                + jnp.take(first, local_map[:, 0], axis=0)
                + jnp.take(second, local_map[:, 1], axis=0)
            )
            state = total.astype(jnp.bfloat16)
        root_solution = product_of(3, state)
        cells_x = adjoint.shape[0]
        cells_y = adjoint.shape[1]
        width = adjoint.shape[2]
        plane = root_solution.reshape(cells_x, cells_y, width)
        stacked = jnp.stack([plane, adjoint])
        padded = padded_2(stacked, ((GX, ngx, 1), ("gy", ngy, 2)), 1)
        padded_u = padded[0]
        padded_a = padded[1]
        gradient = jnp.zeros((cells_x, cells_y, width), jnp.float32)
        for lo_x, lo_y in ((2, 1), (0, 1), (1, 2), (1, 0)):
            near_u = padded_u[lo_x : lo_x + cells_x, lo_y : lo_y + cells_y]
            near_a = padded_a[lo_x : lo_x + cells_x, lo_y : lo_y + cells_y]
            gradient = gradient + (plane - near_u) * (adjoint - near_a)
        return (root_solution, gradient)

    return local


def solution(mesh):
    ngx = mesh.shape["gx"]
    ngy = mesh.shape["gy"]
    nya = 4
    nxa = ngx // (2 * nya)
    devices = np.asarray(mesh.devices).reshape(2, nxa // 2, 2, nya // 2, 2, ngy)
    fine = Mesh(devices, ALL)
    rows = P(ALL, None)
    in_specs = (rows,) * 8 + (P(), P(), P(), P(GX, "gy", None))
    out_specs = (rows, P(GX, "gy", None))
    return jax.shard_map(
        make_local((nxa, nya, ngy)), mesh=fine, in_specs=in_specs, out_specs=out_specs, check_vma=False
    )
```

```python
import numpy as np
import jax
import jax.numpy as jnp
from jax import lax
from jax.sharding import Mesh, PartitionSpec as P

GX = ("xh", "xl", "yh", "yl", "c")
ALL = GX + ("gy",)
YA = ("yh", "yl")
XA = ("xh", "xl")
GROUP = ("xl", "yl", "c")


def moved(x, axis, pairs):
    return lax.ppermute(x, axis, pairs)


def ring_blocks(x, axis, n, size):
    if n == 2 and size != 2:
        got = moved(x, axis, [(i, i ^ 1) for i in range(size)])
        return jnp.stack([x, got]), got
    up = [(i, (i + 1) % n) for i in range(n)]
    down = [(i, (i - 1) % n) for i in range(n)]
    pieces = [None] * n
    pieces[0] = x
    fwd = x
    bwd = x
    for s in range(1, (n - 1) // 2 + 1):
        fwd = moved(fwd, axis, up)
        bwd = moved(bwd, axis, down)
        pieces[n - s] = fwd
        pieces[s] = bwd
    if n % 2 == 0:
        h = x.shape[0] // 2
        a = moved(fwd[:h], axis, up)
        b = moved(bwd[h:], axis, down)
        pieces[n // 2] = jnp.concatenate([a, b], 0)
    return jnp.stack(pieces), pieces[1]


def gather_front(block, dims, order):
    held = []
    x = block
    anchor = None
    for name in order:
        axis, n, size, me = dims[name]
        x, got = ring_blocks(x, axis, n, size)
        anchor = got if anchor is None else anchor
        held.insert(0, name)
    canon = [name for name in ("X", "Y", "Z") if name in dims]
    x = jnp.transpose(x, [held.index(name) for name in canon] + [len(held), len(held) + 1])
    for i, name in enumerate(canon):
        x = jnp.roll(x, dims[name][3], axis=i)
    return x.reshape(-1, x.shape[-1]), anchor


def level_dims(level, sizes, idx):
    nxa, nya, ngy = sizes
    xa, ya, gy = idx
    dims = {"Z": ("gy", ngy, ngy, gy)}
    if level == 0:
        dims["Y"] = (YA, 2, nya, ya % 2)
    else:
        dims["Y"] = (YA, nya, nya, ya)
    if level == 2:
        dims["X"] = (XA, 2, nxa, xa % 2)
    elif level == 3:
        dims["X"] = (XA, nxa, nxa, xa)
    return dims


ORDERS = {
    0: (("Z", "Y"), ("Y", "Z")),
    1: (("Y", "Z"),),
    2: (("Z", "Y", "X"), ("X", "Z", "Y"), ("Y", "X", "Z")),
    3: (("Z", "Y", "X"), ("X", "Z", "Y"), ("Y", "X", "Z")),
}


def split_columns(front, core, groups):
    rows = front.shape[0]
    four = front.reshape(rows, groups, 2, -1)
    mine = lax.dynamic_index_in_dim(four, core, axis=2, keepdims=False).reshape(rows, -1)
    theirs = lax.dynamic_index_in_dim(four, 1 - core, axis=2, keepdims=False).reshape(rows, -1)
    return mine, moved(theirs, "c", [(0, 1), (1, 0)])


def apply_front(prepare, state, level, sizes, idx):
    dims = level_dims(level, sizes, idx)
    orders = ORDERS[level]
    width = state.shape[1]
    count = len(orders)
    edges = [width * i // count // 128 * 128 for i in range(count)] + [width]
    mine = []
    theirs = []
    wholes = []
    anchor = None
    for i, order in enumerate(orders):
        part = state[:, edges[i] : edges[i + 1]]
        whole, got = gather_front(part, dims, order)
        wholes.append(whole)
        anchor = got if anchor is None else anchor
    own_a, other_a = prepare(anchor)
    for whole in wholes:
        mine.append(jnp.dot(own_a, whole, preferred_element_type=jnp.float32))
        theirs.append(jnp.dot(other_a, whole, preferred_element_type=jnp.float32))
    mine = jnp.concatenate(mine, 1)
    theirs = jnp.concatenate(theirs, 1)
    return mine + moved(theirs, "c", [(0, 1), (1, 0)])


def pair_swap(x, axis, size, mask):
    return lax.ppermute(x, axis, [(i, i ^ mask) for i in range(size)])


def spread_front(front, kbits, group, coords):
    rows = front.shape[0]
    names = list(kbits)
    a = front.reshape([rows] + [2] * len(names) + [-1])
    lead = 1
    for axis in group:
        me = coords[axis]
        pos = lead + names.index(axis)
        mine = lax.dynamic_index_in_dim(a, me, axis=pos, keepdims=False)
        theirs = lax.dynamic_index_in_dim(a, 1 - me, axis=pos, keepdims=False)
        got = pair_swap(theirs, axis, 2, 1)
        a = jnp.where(me == 0, jnp.stack([mine, got]), jnp.stack([got, mine]))
        names.remove(axis)
        lead += 1
    return a, names, lead


def doubled(z, steps, coords, sizes):
    cur = z
    for axis, mask, _ in steps:
        got = pair_swap(cur, axis, sizes[axis], mask)
        bit = coords[axis] // mask % 2
        cur = jnp.where(bit == 0, jnp.concatenate([cur, got], 0), jnp.concatenate([got, cur], 0))
    return cur


def apply_grouped(spread, state, steps, group, coords, sizes):
    a, names, lead = spread
    order = [names.index(k) for _, _, k in reversed(steps)]
    perm = list(range(lead)) + [lead + i for i in order] + [lead + len(names)]
    matrix = jnp.transpose(a, perm)
    rows = int(np.prod(matrix.shape[:lead]))
    matrix = matrix.reshape(rows, -1)
    whole = doubled(state, steps, coords, sizes)
    p = jnp.dot(matrix, whole, preferred_element_type=jnp.float32)
    for axis in reversed(group):
        p = p.reshape(2, -1, p.shape[-1])
        me = coords[axis]
        mine = lax.dynamic_index_in_dim(p, me, axis=0, keepdims=False)
        theirs = lax.dynamic_index_in_dim(p, 1 - me, axis=0, keepdims=False)
        p = mine + pair_swap(theirs, axis, 2, 1)
    return p


def padded_2(cells, sides, width):
    for axis, count, dim in sides:
        ends = count - 1
        head = lax.slice_in_dim(cells, 0, width, axis=dim)
        tail = lax.slice_in_dim(cells, cells.shape[dim] - width, cells.shape[dim], axis=dim)
        cells = jnp.concatenate(
            [
                lax.ppermute(tail, axis, [(i, (i + 1) % count) for i in range(ends)]),
                cells,
                lax.ppermute(head, axis, [((i + 1) % count, i) for i in range(ends)]),
            ],
            axis=dim,
        )
    return cells


def make_local(sizes):
    nxa, nya, ngy = sizes
    ngx = nxa * nya * 2
    leaf_bits = ngx.bit_length() - 4

    def local(
        leaf_load,
        front_zero,
        front_one,
        front_two,
        front_root,
        load_one,
        load_two,
        load_root,
        map_one,
        map_two,
        map_root,
        adjoint,
    ):
        fronts = (front_zero, front_one, front_two, front_root)
        loads = (load_one, load_two, load_root)
        mappings = (map_one, map_two, map_root)
        coords = {name: lax.axis_index(name) for name in ALL}
        xa = coords["xh"] * 2 + coords["xl"]
        ya = coords["yh"] * 2 + coords["yl"]
        core = coords["c"]
        row_index = coords["gy"]
        column = (xa * nya + ya) * 2 + core
        idx = (xa, ya, row_index)
        axis_sizes = {name: 2 for name in GX}
        axis_sizes["gy"] = ngy
        gy_bits = [("g%d" % b, 1 << b) for b in reversed(range(ngy.bit_length() - 1))]
        kbits = {
            2: ["xl", "yh", "yl", "c"] + [name for name, _ in gy_bits],
            3: ["xh", "xl", "yh", "yl", "c"] + [name for name, _ in gy_bits],
        }
        high = [("gy",) + tuple(reversed(gy_bits[0]))]
        low = [("gy",) + tuple(reversed(bit)) for bit in gy_bits[1:]]
        steps = {
            2: high + [("yh", 1, "yh")] + low,
            3: high + [("xh", 1, "xh"), ("yh", 1, "yh")] + low,
        }
        parts = {}

        def prepare(anchor):
            tied = lax.optimization_barrier((fronts[0], anchor))[0]
            return split_columns(tied, core, 2)

        def product_of(level, state):
            if level == 0:
                return apply_front(prepare, state, level, sizes, idx)
            if level == 1:
                return apply_front(lambda anchor: parts[1], state, level, sizes, idx)
            return apply_grouped(parts[level], state, steps[level], GROUP, coords, axis_sizes)

        state = leaf_load
        for level in range(3):
            bits = leaf_bits + level
            if level == 2:
                held = (parts[2][0], parts[3][0])
                state, held = lax.optimization_barrier((state, held))
                parts[2] = (held[0],) + parts[2][1:]
                parts[3] = (held[1],) + parts[3][1:]
            product = product_of(level, state)
            if level == 0:
                tied = lax.optimization_barrier((fronts[1:], product))[0]
                parts[1] = split_columns(tied[0], core, nya)
                for later in (2, 3):
                    parts[later] = spread_front(tied[later - 1], kbits[later], GROUP, coords)
            other = moved(product, GX, [(i, i ^ 1 << bits) for i in range(ngx)])
            upper = column >> bits & 1 == 1
            first = jnp.where(upper, other, product)
            second = jnp.where(upper, product, other)
            half = product.shape[0] // 2
            position = column % 2 ** (bits + 1) * ngy + row_index
            local_map = lax.dynamic_slice_in_dim(mappings[level], position * half, half, 0)
            total = (
                loads[level]
                + jnp.take(first, local_map[:, 0], axis=0)
                + jnp.take(second, local_map[:, 1], axis=0)
            )
            state = total.astype(jnp.bfloat16)
        root_solution = product_of(3, state)
        cells_x = adjoint.shape[0]
        cells_y = adjoint.shape[1]
        width = adjoint.shape[2]
        plane = root_solution.reshape(cells_x, cells_y, width)
        stacked = jnp.stack([plane, adjoint])
        padded = padded_2(stacked, ((GX, ngx, 1), ("gy", ngy, 2)), 1)
        padded_u = padded[0]
        padded_a = padded[1]
        gradient = jnp.zeros((cells_x, cells_y, width), jnp.float32)
        for lo_x, lo_y in ((2, 1), (0, 1), (1, 2), (1, 0)):
            near_u = padded_u[lo_x : lo_x + cells_x, lo_y : lo_y + cells_y]
            near_a = padded_a[lo_x : lo_x + cells_x, lo_y : lo_y + cells_y]
            gradient = gradient + (plane - near_u) * (adjoint - near_a)
        return (root_solution, gradient)

    return local


def solution(mesh):
    ngx = mesh.shape["gx"]
    ngy = mesh.shape["gy"]
    nya = 4
    nxa = ngx // (2 * nya)
    devices = np.asarray(mesh.devices).reshape(2, nxa // 2, 2, nya // 2, 2, ngy)
    fine = Mesh(devices, ALL)
    rows = P(ALL, None)
    in_specs = (rows,) * 8 + (P(), P(), P(), P(GX, "gy", None))
    out_specs = (rows, P(GX, "gy", None))
    return jax.shard_map(
        make_local((nxa, nya, ngy)), mesh=fine, in_specs=in_specs, out_specs=out_specs, check_vma=False
    )
```

```python
import numpy as np
import jax
import jax.numpy as jnp
from jax import lax
from jax.sharding import Mesh, PartitionSpec as P

GX = ("xh", "xl", "yh", "yl", "c")
ALL = GX + ("gy",)
YA = ("yh", "yl")
XA = ("xh", "xl")
GROUP = ("xl", "yl", "c")


def moved(x, axis, pairs):
    return lax.ppermute(x, axis, pairs)


def ring_blocks(x, axis, n, size):
    if n == 2 and size != 2:
        got = moved(x, axis, [(i, i ^ 1) for i in range(size)])
        return jnp.stack([x, got]), got
    up = [(i, (i + 1) % n) for i in range(n)]
    down = [(i, (i - 1) % n) for i in range(n)]
    pieces = [None] * n
    pieces[0] = x
    fwd = x
    bwd = x
    for s in range(1, (n - 1) // 2 + 1):
        fwd = moved(fwd, axis, up)
        bwd = moved(bwd, axis, down)
        pieces[n - s] = fwd
        pieces[s] = bwd
    if n % 2 == 0:
        h = x.shape[0] // 2
        a = moved(fwd[:h], axis, up)
        b = moved(bwd[h:], axis, down)
        pieces[n // 2] = jnp.concatenate([a, b], 0)
    return jnp.stack(pieces), pieces[1]


def gather_front(block, dims, order):
    held = []
    x = block
    anchor = None
    for name in order:
        axis, n, size, me = dims[name]
        x, got = ring_blocks(x, axis, n, size)
        anchor = got if anchor is None else anchor
        held.insert(0, name)
    canon = [name for name in ("X", "Y", "Z") if name in dims]
    x = jnp.transpose(x, [held.index(name) for name in canon] + [len(held), len(held) + 1])
    for i, name in enumerate(canon):
        x = jnp.roll(x, dims[name][3], axis=i)
    return x.reshape(-1, x.shape[-1]), anchor


def level_dims(level, sizes, idx):
    nxa, nya, ngy = sizes
    xa, ya, gy = idx
    dims = {"Z": ("gy", ngy, ngy, gy)}
    if level == 0:
        dims["Y"] = (YA, 2, nya, ya % 2)
    else:
        dims["Y"] = (YA, nya, nya, ya)
    if level == 2:
        dims["X"] = (XA, 2, nxa, xa % 2)
    elif level == 3:
        dims["X"] = (XA, nxa, nxa, xa)
    return dims


ORDERS = {
    0: (("Z", "Y"), ("Y", "Z")),
    1: (("Y", "Z"),),
    2: (("Z", "Y", "X"), ("X", "Z", "Y"), ("Y", "X", "Z")),
    3: (("Z", "Y", "X"), ("X", "Z", "Y"), ("Y", "X", "Z")),
}


def split_columns(front, core, groups):
    rows = front.shape[0]
    four = front.reshape(rows, groups, 2, -1)
    mine = lax.dynamic_index_in_dim(four, core, axis=2, keepdims=False).reshape(rows, -1)
    theirs = lax.dynamic_index_in_dim(four, 1 - core, axis=2, keepdims=False).reshape(rows, -1)
    return mine, moved(theirs, "c", [(0, 1), (1, 0)])


def apply_front(prepare, state, level, sizes, idx):
    dims = level_dims(level, sizes, idx)
    orders = ORDERS[level]
    width = state.shape[1]
    count = len(orders)
    edges = [width * i // count // 128 * 128 for i in range(count)] + [width]
    mine = []
    theirs = []
    wholes = []
    anchor = None
    for i, order in enumerate(orders):
        part = state[:, edges[i] : edges[i + 1]]
        whole, got = gather_front(part, dims, order)
        wholes.append(whole)
        anchor = got if anchor is None else anchor
    own_a, other_a = prepare(anchor)
    for whole in wholes:
        mine.append(jnp.dot(own_a, whole, preferred_element_type=jnp.float32))
        theirs.append(jnp.dot(other_a, whole, preferred_element_type=jnp.float32))
    mine = jnp.concatenate(mine, 1)
    theirs = jnp.concatenate(theirs, 1)
    return mine + moved(theirs, "c", [(0, 1), (1, 0)])


def pair_swap(x, axis, size, mask):
    return lax.ppermute(x, axis, [(i, i ^ mask) for i in range(size)])


def spread_front(front, kbits, group, coords):
    rows = front.shape[0]
    names = list(kbits)
    a = front.reshape([rows] + [2] * len(names) + [-1])
    lead = 1
    for axis in group:
        me = coords[axis]
        pos = lead + names.index(axis)
        mine = lax.dynamic_index_in_dim(a, me, axis=pos, keepdims=False)
        theirs = lax.dynamic_index_in_dim(a, 1 - me, axis=pos, keepdims=False)
        got = pair_swap(theirs, axis, 2, 1)
        a = jnp.where(me == 0, jnp.stack([mine, got]), jnp.stack([got, mine]))
        names.remove(axis)
        lead += 1
    return a, names, lead


def doubled(z, steps, coords, sizes):
    cur = z
    for axis, mask, _ in steps:
        got = pair_swap(cur, axis, sizes[axis], mask)
        bit = coords[axis] // mask % 2
        cur = jnp.where(bit == 0, jnp.concatenate([cur, got], 0), jnp.concatenate([got, cur], 0))
    return cur


def grouped_matrix(spread, steps):
    a, names, lead = spread
    order = [names.index(k) for _, _, k in reversed(steps)]
    perm = list(range(lead)) + [lead + i for i in order] + [lead + len(names)]
    matrix = jnp.transpose(a, perm)
    rows = int(np.prod(matrix.shape[:lead]))
    return matrix.reshape(rows, -1)


def apply_grouped(matrix, state, steps, group, coords, sizes):
    whole = doubled(state, steps, coords, sizes)
    p = jnp.dot(matrix, whole, preferred_element_type=jnp.float32)
    for axis in reversed(group):
        p = p.reshape(2, -1, p.shape[-1])
        me = coords[axis]
        mine = lax.dynamic_index_in_dim(p, me, axis=0, keepdims=False)
        theirs = lax.dynamic_index_in_dim(p, 1 - me, axis=0, keepdims=False)
        p = mine + pair_swap(theirs, axis, 2, 1)
    return p


def halo(cells, axis, count, dim):
    size = cells.shape[dim]
    head = lax.slice_in_dim(cells, 0, 1, axis=dim)
    tail = lax.slice_in_dim(cells, size - 1, size, axis=dim)
    below = lax.ppermute(tail, axis, [(i, i + 1) for i in range(count - 1)])
    above = lax.ppermute(head, axis, [(i + 1, i) for i in range(count - 1)])
    inner_lo = lax.slice_in_dim(cells, 0, size - 1, axis=dim)
    inner_hi = lax.slice_in_dim(cells, 1, size, axis=dim)
    return jnp.concatenate([below, inner_lo], dim), jnp.concatenate([inner_hi, above], dim)


def make_local(sizes):
    nxa, nya, ngy = sizes
    ngx = nxa * nya * 2
    leaf_bits = ngx.bit_length() - 4

    def local(
        leaf_load,
        front_zero,
        front_one,
        front_two,
        front_root,
        load_one,
        load_two,
        load_root,
        map_one,
        map_two,
        map_root,
        adjoint,
    ):
        fronts = (front_zero, front_one, front_two, front_root)
        loads = (load_one, load_two, load_root)
        mappings = (map_one, map_two, map_root)
        coords = {name: lax.axis_index(name) for name in ALL}
        xa = coords["xh"] * 2 + coords["xl"]
        ya = coords["yh"] * 2 + coords["yl"]
        core = coords["c"]
        row_index = coords["gy"]
        column = (xa * nya + ya) * 2 + core
        idx = (xa, ya, row_index)
        axis_sizes = {name: 2 for name in GX}
        axis_sizes["gy"] = ngy
        gy_bits = [("g%d" % b, 1 << b) for b in reversed(range(ngy.bit_length() - 1))]
        kbits = {
            2: ["xl", "yh", "yl", "c"] + [name for name, _ in gy_bits],
            3: ["xh", "xl", "yh", "yl", "c"] + [name for name, _ in gy_bits],
        }
        high = [("gy",) + tuple(reversed(gy_bits[0]))]
        low = [("gy",) + tuple(reversed(bit)) for bit in gy_bits[1:]]
        steps = {
            2: high + [("yh", 1, "yh")] + low,
            3: high + [("xh", 1, "xh"), ("yh", 1, "yh")] + low,
        }
        parts = {}

        def prepare(anchor):
            tied = lax.optimization_barrier((fronts[0], anchor))[0]
            return split_columns(tied, core, 2)

        def product_of(level, state):
            if level == 0:
                return apply_front(prepare, state, level, sizes, idx)
            if level == 1:
                return apply_front(lambda anchor: parts[1], state, level, sizes, idx)
            return apply_grouped(parts[level], state, steps[level], GROUP, coords, axis_sizes)

        state = leaf_load
        for level in range(3):
            bits = leaf_bits + level
            if level == 2:
                state, held = lax.optimization_barrier((state, (parts[2], parts[3])))
                parts[2], parts[3] = held
            product = product_of(level, state)
            if level == 0:
                tied = lax.optimization_barrier((fronts[1:], product))[0]
                parts[1] = split_columns(tied[0], core, nya)
                for later in (2, 3):
                    spread = spread_front(tied[later - 1], kbits[later], GROUP, coords)
                    parts[later] = grouped_matrix(spread, steps[later])
            other = moved(product, GX, [(i, i ^ 1 << bits) for i in range(ngx)])
            upper = column >> bits & 1 == 1
            first = jnp.where(upper, other, product)
            second = jnp.where(upper, product, other)
            half = product.shape[0] // 2
            position = column % 2 ** (bits + 1) * ngy + row_index
            local_map = lax.dynamic_slice_in_dim(mappings[level], position * half, half, 0)
            total = (
                loads[level]
                + jnp.take(first, local_map[:, 0], axis=0)
                + jnp.take(second, local_map[:, 1], axis=0)
            )
            state = total.astype(jnp.bfloat16)
        root_solution = product_of(3, state)
        cells_x = adjoint.shape[0]
        cells_y = adjoint.shape[1]
        width = adjoint.shape[2]
        plane = root_solution.reshape(cells_x, cells_y, width)
        gradient = jnp.zeros((cells_x, cells_y, width), jnp.float32)
        for dim, axis, count in ((0, GX, ngx), (1, "gy", ngy)):
            u_lo, u_hi = halo(plane, axis, count, dim)
            a_lo, a_hi = halo(adjoint, axis, count, dim)
            gradient = gradient + (plane - u_hi) * (adjoint - a_hi)
            gradient = gradient + (plane - u_lo) * (adjoint - a_lo)
        return (root_solution, gradient)

    return local


def solution(mesh):
    ngx = mesh.shape["gx"]
    ngy = mesh.shape["gy"]
    nya = 4
    nxa = ngx // (2 * nya)
    devices = np.asarray(mesh.devices).reshape(2, nxa // 2, 2, nya // 2, 2, ngy)
    fine = Mesh(devices, ALL)
    rows = P(ALL, None)
    in_specs = (rows,) * 8 + (P(), P(), P(), P(GX, "gy", None))
    out_specs = (rows, P(GX, "gy", None))
    return jax.shard_map(
        make_local((nxa, nya, ngy)), mesh=fine, in_specs=in_specs, out_specs=out_specs, check_vma=False
    )
```

```python
import numpy as np
import jax
import jax.numpy as jnp
from jax import lax
from jax.sharding import Mesh, PartitionSpec as P

GX = ("xh", "xl", "yh", "yl", "c")
ALL = GX + ("gy",)
YA = ("yh", "yl")
XA = ("xh", "xl")
GROUP = ("xl", "yl", "c")


def moved(x, axis, pairs):
    return lax.ppermute(x, axis, pairs)


def ring_blocks(x, axis, n, size):
    if n == 2 and size != 2:
        got = moved(x, axis, [(i, i ^ 1) for i in range(size)])
        return jnp.stack([x, got]), got
    up = [(i, (i + 1) % n) for i in range(n)]
    down = [(i, (i - 1) % n) for i in range(n)]
    pieces = [None] * n
    pieces[0] = x
    fwd = x
    bwd = x
    for s in range(1, (n - 1) // 2 + 1):
        fwd = moved(fwd, axis, up)
        bwd = moved(bwd, axis, down)
        pieces[n - s] = fwd
        pieces[s] = bwd
    if n % 2 == 0:
        h = x.shape[0] // 2
        a = moved(fwd[:h], axis, up)
        b = moved(bwd[h:], axis, down)
        pieces[n // 2] = jnp.concatenate([a, b], 0)
    return jnp.stack(pieces), pieces[1]


def gather_front(block, dims, order):
    held = []
    x = block
    anchor = None
    for name in order:
        axis, n, size, me = dims[name]
        x, got = ring_blocks(x, axis, n, size)
        anchor = got if anchor is None else anchor
        held.insert(0, name)
    canon = [name for name in ("X", "Y", "Z") if name in dims]
    x = jnp.transpose(x, [held.index(name) for name in canon] + [len(held), len(held) + 1])
    for i, name in enumerate(canon):
        x = jnp.roll(x, dims[name][3], axis=i)
    return x.reshape(-1, x.shape[-1]), anchor


def level_dims(level, sizes, idx):
    nxa, nya, ngy = sizes
    xa, ya, gy = idx
    dims = {"Z": ("gy", ngy, ngy, gy)}
    if level == 0:
        dims["Y"] = (YA, 2, nya, ya % 2)
    else:
        dims["Y"] = (YA, nya, nya, ya)
    if level == 2:
        dims["X"] = (XA, 2, nxa, xa % 2)
    elif level == 3:
        dims["X"] = (XA, nxa, nxa, xa)
    return dims


ORDERS = {
    0: (("Z", "Y"), ("Y", "Z")),
    1: (("Y", "Z"),),
    2: (("Z", "Y", "X"), ("X", "Z", "Y"), ("Y", "X", "Z")),
    3: (("Z", "Y", "X"), ("X", "Z", "Y"), ("Y", "X", "Z")),
}


def split_columns(front, core, groups):
    rows = front.shape[0]
    four = front.reshape(rows, groups, 2, -1)
    mine = lax.dynamic_index_in_dim(four, core, axis=2, keepdims=False).reshape(rows, -1)
    theirs = lax.dynamic_index_in_dim(four, 1 - core, axis=2, keepdims=False).reshape(rows, -1)
    return mine, moved(theirs, "c", [(0, 1), (1, 0)])


def apply_front(prepare, state, level, sizes, idx):
    dims = level_dims(level, sizes, idx)
    orders = ORDERS[level]
    width = state.shape[1]
    count = len(orders)
    edges = [width * i // count // 128 * 128 for i in range(count)] + [width]
    mine = []
    theirs = []
    wholes = []
    anchor = None
    for i, order in enumerate(orders):
        part = state[:, edges[i] : edges[i + 1]]
        whole, got = gather_front(part, dims, order)
        wholes.append(whole)
        anchor = got if anchor is None else anchor
    own_a, other_a = prepare(anchor)
    for whole in wholes:
        mine.append(jnp.dot(own_a, whole, preferred_element_type=jnp.float32))
        theirs.append(jnp.dot(other_a, whole, preferred_element_type=jnp.float32))
    mine = jnp.concatenate(mine, 1)
    theirs = jnp.concatenate(theirs, 1)
    return mine + moved(theirs, "c", [(0, 1), (1, 0)])


def pair_swap(x, axis, size, mask):
    return lax.ppermute(x, axis, [(i, i ^ mask) for i in range(size)])


def spread_front(front, kbits, group, coords):
    rows = front.shape[0]
    names = list(kbits)
    a = front.reshape([rows] + [2] * len(names) + [-1])
    lead = 1
    for axis in group:
        me = coords[axis]
        pos = lead + names.index(axis)
        mine = lax.dynamic_index_in_dim(a, me, axis=pos, keepdims=False)
        theirs = lax.dynamic_index_in_dim(a, 1 - me, axis=pos, keepdims=False)
        got = pair_swap(theirs, axis, 2, 1)
        a = jnp.where(me == 0, jnp.stack([mine, got]), jnp.stack([got, mine]))
        names.remove(axis)
        lead += 1
    return a, names, lead


def doubled(z, steps, coords, sizes):
    cur = z
    for axis, mask, _ in steps:
        got = pair_swap(cur, axis, sizes[axis], mask)
        bit = coords[axis] // mask % 2
        cur = jnp.where(bit == 0, jnp.concatenate([cur, got], 0), jnp.concatenate([got, cur], 0))
    return cur


def grouped_matrix(spread, steps):
    a, names, lead = spread
    order = [names.index(k) for _, _, k in reversed(steps)]
    perm = list(range(lead)) + [lead + i for i in order] + [lead + len(names)]
    matrix = jnp.transpose(a, perm)
    rows = int(np.prod(matrix.shape[:lead]))
    return matrix.reshape(rows, -1)


def apply_grouped(matrix, state, steps, group, coords, sizes):
    whole = doubled(state, steps, coords, sizes)
    p = jnp.dot(matrix, whole, preferred_element_type=jnp.float32)
    for axis in reversed(group):
        p = p.reshape(2, -1, p.shape[-1])
        me = coords[axis]
        mine = lax.dynamic_index_in_dim(p, me, axis=0, keepdims=False)
        theirs = lax.dynamic_index_in_dim(p, 1 - me, axis=0, keepdims=False)
        p = mine + pair_swap(theirs, axis, 2, 1)
    return p


def halo(cells, axis, count, dim):
    size = cells.shape[dim]
    head = lax.slice_in_dim(cells, 0, 1, axis=dim)
    tail = lax.slice_in_dim(cells, size - 1, size, axis=dim)
    below = lax.ppermute(tail, axis, [(i, i + 1) for i in range(count - 1)])
    above = lax.ppermute(head, axis, [(i + 1, i) for i in range(count - 1)])
    inner_lo = lax.slice_in_dim(cells, 0, size - 1, axis=dim)
    inner_hi = lax.slice_in_dim(cells, 1, size, axis=dim)
    return jnp.concatenate([below, inner_lo], dim), jnp.concatenate([inner_hi, above], dim)


def make_local(sizes):
    nxa, nya, ngy = sizes
    ngx = nxa * nya * 2
    leaf_bits = ngx.bit_length() - 4

    def local(
        leaf_load,
        front_zero,
        front_one,
        front_two,
        front_root,
        load_one,
        load_two,
        load_root,
        map_one,
        map_two,
        map_root,
        adjoint,
    ):
        fronts = (front_zero, front_one, front_two, front_root)
        loads = (load_one, load_two, load_root)
        mappings = (map_one, map_two, map_root)
        coords = {name: lax.axis_index(name) for name in ALL}
        xa = coords["xh"] * 2 + coords["xl"]
        ya = coords["yh"] * 2 + coords["yl"]
        core = coords["c"]
        row_index = coords["gy"]
        column = (xa * nya + ya) * 2 + core
        idx = (xa, ya, row_index)
        axis_sizes = {name: 2 for name in GX}
        axis_sizes["gy"] = ngy
        gy_bits = [("g%d" % b, 1 << b) for b in reversed(range(ngy.bit_length() - 1))]
        kbits = {
            2: ["xl", "yh", "yl", "c"] + [name for name, _ in gy_bits],
            3: ["xh", "xl", "yh", "yl", "c"] + [name for name, _ in gy_bits],
        }
        high = [("gy",) + tuple(reversed(gy_bits[0]))]
        low = [("gy",) + tuple(reversed(bit)) for bit in gy_bits[1:]]
        steps = {
            2: high + [("yh", 1, "yh")] + low,
            3: high + [("xh", 1, "xh"), ("yh", 1, "yh")] + low,
        }
        parts = {}

        def prepare(anchor):
            tied = lax.optimization_barrier((fronts[0], anchor))[0]
            return split_columns(tied, core, 2)

        def product_of(level, state):
            if level == 0:
                return apply_front(prepare, state, level, sizes, idx)
            if level == 1:
                return apply_front(lambda anchor: parts[1], state, level, sizes, idx)
            matrix = grouped_matrix(parts[level], steps[level])
            return apply_grouped(matrix, state, steps[level], GROUP, coords, axis_sizes)

        state = leaf_load
        for level in range(3):
            bits = leaf_bits + level
            if level == 2:
                state, held = lax.optimization_barrier((state, (parts[2][0], parts[3][0])))
                parts[2] = (held[0],) + parts[2][1:]
                parts[3] = (held[1],) + parts[3][1:]
            product = product_of(level, state)
            if level == 0:
                tied = lax.optimization_barrier((fronts[1:], product))[0]
                parts[1] = split_columns(tied[0], core, nya)
                for later in (2, 3):
                    parts[later] = spread_front(tied[later - 1], kbits[later], GROUP, coords)
            other = moved(product, GX, [(i, i ^ 1 << bits) for i in range(ngx)])
            upper = column >> bits & 1 == 1
            first = jnp.where(upper, other, product)
            second = jnp.where(upper, product, other)
            half = product.shape[0] // 2
            position = column % 2 ** (bits + 1) * ngy + row_index
            local_map = lax.dynamic_slice_in_dim(mappings[level], position * half, half, 0)
            total = (
                loads[level]
                + jnp.take(first, local_map[:, 0], axis=0)
                + jnp.take(second, local_map[:, 1], axis=0)
            )
            state = total.astype(jnp.bfloat16)
        root_solution = product_of(3, state)
        cells_x = adjoint.shape[0]
        cells_y = adjoint.shape[1]
        width = adjoint.shape[2]
        plane = root_solution.reshape(cells_x, cells_y, width)
        gradient = jnp.zeros((cells_x, cells_y, width), jnp.float32)
        for dim, axis, count in ((0, GX, ngx), (1, "gy", ngy)):
            u_lo, u_hi = halo(plane, axis, count, dim)
            a_lo, a_hi = halo(adjoint, axis, count, dim)
            gradient = gradient + (plane - u_hi) * (adjoint - a_hi)
            gradient = gradient + (plane - u_lo) * (adjoint - a_lo)
        return (root_solution, gradient)

    return local


def solution(mesh):
    ngx = mesh.shape["gx"]
    ngy = mesh.shape["gy"]
    nya = 4
    nxa = ngx // (2 * nya)
    devices = np.asarray(mesh.devices).reshape(2, nxa // 2, 2, nya // 2, 2, ngy)
    fine = Mesh(devices, ALL)
    rows = P(ALL, None)
    in_specs = (rows,) * 8 + (P(), P(), P(), P(GX, "gy", None))
    out_specs = (rows, P(GX, "gy", None))
    return jax.shard_map(
        make_local((nxa, nya, ngy)), mesh=fine, in_specs=in_specs, out_specs=out_specs, check_vma=False
    )
```

```python
import numpy as np
import jax
import jax.numpy as jnp
from jax import lax
from jax.sharding import Mesh, PartitionSpec as P

GX = ("xh", "xl", "yh", "yl", "c")
ALL = GX + ("gy",)
YA = ("yh", "yl")
XA = ("xh", "xl")
GROUP = ("xl", "yl", "c")


def moved(x, axis, pairs):
    return lax.ppermute(x, axis, pairs)


def ring_blocks(x, axis, n, size):
    if n == 2 and size != 2:
        got = moved(x, axis, [(i, i ^ 1) for i in range(size)])
        return jnp.stack([x, got]), got
    up = [(i, (i + 1) % n) for i in range(n)]
    down = [(i, (i - 1) % n) for i in range(n)]
    pieces = [None] * n
    pieces[0] = x
    fwd = x
    bwd = x
    for s in range(1, (n - 1) // 2 + 1):
        fwd = moved(fwd, axis, up)
        bwd = moved(bwd, axis, down)
        pieces[n - s] = fwd
        pieces[s] = bwd
    if n % 2 == 0:
        h = x.shape[0] // 2
        a = moved(fwd[:h], axis, up)
        b = moved(bwd[h:], axis, down)
        pieces[n // 2] = jnp.concatenate([a, b], 0)
    return jnp.stack(pieces), pieces[1]


def gather_front(block, dims, order):
    held = []
    x = block
    anchor = None
    for name in order:
        axis, n, size, me = dims[name]
        x, got = ring_blocks(x, axis, n, size)
        anchor = got if anchor is None else anchor
        held.insert(0, name)
    canon = [name for name in ("X", "Y", "Z") if name in dims]
    x = jnp.transpose(x, [held.index(name) for name in canon] + [len(held), len(held) + 1])
    for i, name in enumerate(canon):
        x = jnp.roll(x, dims[name][3], axis=i)
    return x.reshape(-1, x.shape[-1]), anchor


def level_dims(level, sizes, idx):
    nxa, nya, ngy = sizes
    xa, ya, gy = idx
    dims = {"Z": ("gy", ngy, ngy, gy)}
    if level == 0:
        dims["Y"] = (YA, 2, nya, ya % 2)
    else:
        dims["Y"] = (YA, nya, nya, ya)
    if level == 2:
        dims["X"] = (XA, 2, nxa, xa % 2)
    elif level == 3:
        dims["X"] = (XA, nxa, nxa, xa)
    return dims


ORDERS = {
    0: (("Z", "Y"), ("Y", "Z")),
    1: (("Z", "Y"), ("Y", "Z")),
    2: (("Z", "Y", "X"), ("X", "Z", "Y"), ("Y", "X", "Z")),
    3: (("Z", "Y", "X"), ("X", "Z", "Y"), ("Y", "X", "Z")),
}


def split_columns(front, core, groups):
    rows = front.shape[0]
    four = front.reshape(rows, groups, 2, -1)
    mine = lax.dynamic_index_in_dim(four, core, axis=2, keepdims=False).reshape(rows, -1)
    theirs = lax.dynamic_index_in_dim(four, 1 - core, axis=2, keepdims=False).reshape(rows, -1)
    return mine, moved(theirs, "c", [(0, 1), (1, 0)])


def apply_front(prepare, state, level, sizes, idx):
    dims = level_dims(level, sizes, idx)
    orders = ORDERS[level]
    width = state.shape[1]
    count = len(orders)
    edges = [width * i // count // 128 * 128 for i in range(count)] + [width]
    mine = []
    theirs = []
    wholes = []
    anchor = None
    for i, order in enumerate(orders):
        part = state[:, edges[i] : edges[i + 1]]
        whole, got = gather_front(part, dims, order)
        wholes.append(whole)
        anchor = got if anchor is None else anchor
    own_a, other_a = prepare(anchor)
    for whole in wholes:
        mine.append(jnp.dot(own_a, whole, preferred_element_type=jnp.float32))
        theirs.append(jnp.dot(other_a, whole, preferred_element_type=jnp.float32))
    mine = jnp.concatenate(mine, 1)
    theirs = jnp.concatenate(theirs, 1)
    return mine + moved(theirs, "c", [(0, 1), (1, 0)])


def pair_swap(x, axis, size, mask):
    return lax.ppermute(x, axis, [(i, i ^ mask) for i in range(size)])


def spread_front(front, kbits, group, coords):
    rows = front.shape[0]
    names = list(kbits)
    a = front.reshape([rows] + [2] * len(names) + [-1])
    lead = 1
    for axis in group:
        me = coords[axis]
        pos = lead + names.index(axis)
        mine = lax.dynamic_index_in_dim(a, me, axis=pos, keepdims=False)
        theirs = lax.dynamic_index_in_dim(a, 1 - me, axis=pos, keepdims=False)
        got = pair_swap(theirs, axis, 2, 1)
        a = jnp.where(me == 0, jnp.stack([mine, got]), jnp.stack([got, mine]))
        names.remove(axis)
        lead += 1
    return a, names, lead


def doubled(z, steps, coords, sizes):
    cur = z
    for axis, mask, _ in steps:
        got = pair_swap(cur, axis, sizes[axis], mask)
        bit = coords[axis] // mask % 2
        cur = jnp.where(bit == 0, jnp.concatenate([cur, got], 0), jnp.concatenate([got, cur], 0))
    return cur


def apply_grouped(spread, state, steps, group, coords, sizes):
    a, names, lead = spread
    order = [names.index(k) for _, _, k in reversed(steps)]
    perm = list(range(lead)) + [lead + i for i in order] + [lead + len(names)]
    matrix = jnp.transpose(a, perm)
    rows = int(np.prod(matrix.shape[:lead]))
    matrix = matrix.reshape(rows, -1)
    whole = doubled(state, steps, coords, sizes)
    p = jnp.dot(matrix, whole, preferred_element_type=jnp.float32)
    for axis in reversed(group):
        p = p.reshape(2, -1, p.shape[-1])
        me = coords[axis]
        mine = lax.dynamic_index_in_dim(p, me, axis=0, keepdims=False)
        theirs = lax.dynamic_index_in_dim(p, 1 - me, axis=0, keepdims=False)
        p = mine + pair_swap(theirs, axis, 2, 1)
    return p


def padded_2(cells, sides, width):
    for axis, count, dim in sides:
        ends = count - 1
        head = lax.slice_in_dim(cells, 0, width, axis=dim)
        tail = lax.slice_in_dim(cells, cells.shape[dim] - width, cells.shape[dim], axis=dim)
        cells = jnp.concatenate(
            [
                lax.ppermute(tail, axis, [(i, (i + 1) % count) for i in range(ends)]),
                cells,
                lax.ppermute(head, axis, [((i + 1) % count, i) for i in range(ends)]),
            ],
            axis=dim,
        )
    return cells


def make_local(sizes):
    nxa, nya, ngy = sizes
    ngx = nxa * nya * 2
    leaf_bits = ngx.bit_length() - 4

    def local(
        leaf_load,
        front_zero,
        front_one,
        front_two,
        front_root,
        load_one,
        load_two,
        load_root,
        map_one,
        map_two,
        map_root,
        adjoint,
    ):
        fronts = (front_zero, front_one, front_two, front_root)
        loads = (load_one, load_two, load_root)
        mappings = (map_one, map_two, map_root)
        coords = {name: lax.axis_index(name) for name in ALL}
        xa = coords["xh"] * 2 + coords["xl"]
        ya = coords["yh"] * 2 + coords["yl"]
        core = coords["c"]
        row_index = coords["gy"]
        column = (xa * nya + ya) * 2 + core
        idx = (xa, ya, row_index)
        axis_sizes = {name: 2 for name in GX}
        axis_sizes["gy"] = ngy
        gy_bits = [("g%d" % b, 1 << b) for b in reversed(range(ngy.bit_length() - 1))]
        kbits = {
            2: ["xl", "yh", "yl", "c"] + [name for name, _ in gy_bits],
            3: ["xh", "xl", "yh", "yl", "c"] + [name for name, _ in gy_bits],
        }
        high = [("gy",) + tuple(reversed(gy_bits[0]))]
        low = [("gy",) + tuple(reversed(bit)) for bit in gy_bits[1:]]
        steps = {
            2: high + [("yh", 1, "yh")] + low,
            3: high + [("xh", 1, "xh"), ("yh", 1, "yh")] + low,
        }
        parts = {}

        def prepare(anchor):
            tied = lax.optimization_barrier((fronts[0], anchor))[0]
            return split_columns(tied, core, 2)

        def product_of(level, state):
            if level == 0:
                return apply_front(prepare, state, level, sizes, idx)
            if level == 1:
                return apply_front(lambda anchor: parts[1], state, level, sizes, idx)
            return apply_grouped(parts[level], state, steps[level], GROUP, coords, axis_sizes)

        state = leaf_load
        for level in range(3):
            bits = leaf_bits + level
            if level == 2:
                held = (parts[2][0], parts[3][0])
                state, held = lax.optimization_barrier((state, held))
                parts[2] = (held[0],) + parts[2][1:]
                parts[3] = (held[1],) + parts[3][1:]
            product = product_of(level, state)
            if level == 0:
                tied = lax.optimization_barrier((fronts[1:], product))[0]
                parts[1] = split_columns(tied[0], core, nya)
                for later in (2, 3):
                    parts[later] = spread_front(tied[later - 1], kbits[later], GROUP, coords)
            other = moved(product, GX, [(i, i ^ 1 << bits) for i in range(ngx)])
            upper = column >> bits & 1 == 1
            first = jnp.where(upper, other, product)
            second = jnp.where(upper, product, other)
            half = product.shape[0] // 2
            position = column % 2 ** (bits + 1) * ngy + row_index
            local_map = lax.dynamic_slice_in_dim(mappings[level], position * half, half, 0)
            total = (
                loads[level]
                + jnp.take(first, local_map[:, 0], axis=0)
                + jnp.take(second, local_map[:, 1], axis=0)
            )
            state = total.astype(jnp.bfloat16)
        root_solution = product_of(3, state)
        cells_x = adjoint.shape[0]
        cells_y = adjoint.shape[1]
        width = adjoint.shape[2]
        plane = root_solution.reshape(cells_x, cells_y, width)
        stacked = jnp.stack([plane, adjoint])
        padded = padded_2(stacked, ((GX, ngx, 1), ("gy", ngy, 2)), 1)
        padded_u = padded[0]
        padded_a = padded[1]
        gradient = jnp.zeros((cells_x, cells_y, width), jnp.float32)
        for lo_x, lo_y in ((2, 1), (0, 1), (1, 2), (1, 0)):
            near_u = padded_u[lo_x : lo_x + cells_x, lo_y : lo_y + cells_y]
            near_a = padded_a[lo_x : lo_x + cells_x, lo_y : lo_y + cells_y]
            gradient = gradient + (plane - near_u) * (adjoint - near_a)
        return (root_solution, gradient)

    return local


def solution(mesh):
    ngx = mesh.shape["gx"]
    ngy = mesh.shape["gy"]
    nya = 4
    nxa = ngx // (2 * nya)
    devices = np.asarray(mesh.devices).reshape(2, nxa // 2, 2, nya // 2, 2, ngy)
    fine = Mesh(devices, ALL)
    rows = P(ALL, None)
    in_specs = (rows,) * 8 + (P(), P(), P(), P(GX, "gy", None))
    out_specs = (rows, P(GX, "gy", None))
    return jax.shard_map(
        make_local((nxa, nya, ngy)), mesh=fine, in_specs=in_specs, out_specs=out_specs, check_vma=False
    )
```

```python
import numpy as np
import jax
import jax.numpy as jnp
from jax import lax
from jax.sharding import Mesh, PartitionSpec as P

GX = ("xh", "xl", "yh", "yl", "c")
ALL = GX + ("gy",)
YA = ("yh", "yl")
XA = ("xh", "xl")
GROUP = ("xl", "yl", "c")


def moved(x, axis, pairs):
    return lax.ppermute(x, axis, pairs)


def ring_blocks(x, axis, n, size):
    if n == 2 and size != 2:
        got = moved(x, axis, [(i, i ^ 1) for i in range(size)])
        return jnp.stack([x, got]), got
    up = [(i, (i + 1) % n) for i in range(n)]
    down = [(i, (i - 1) % n) for i in range(n)]
    pieces = [None] * n
    pieces[0] = x
    fwd = x
    bwd = x
    for s in range(1, (n - 1) // 2 + 1):
        fwd = moved(fwd, axis, up)
        bwd = moved(bwd, axis, down)
        pieces[n - s] = fwd
        pieces[s] = bwd
    if n % 2 == 0:
        h = x.shape[0] // 2
        a = moved(fwd[:h], axis, up)
        b = moved(bwd[h:], axis, down)
        pieces[n // 2] = jnp.concatenate([a, b], 0)
    return jnp.stack(pieces), pieces[1]


def gather_front(block, dims, order):
    held = []
    x = block
    anchor = None
    for name in order:
        axis, n, size, me = dims[name]
        x, got = ring_blocks(x, axis, n, size)
        anchor = got if anchor is None else anchor
        held.insert(0, name)
    canon = [name for name in ("X", "Y", "Z") if name in dims]
    x = jnp.transpose(x, [held.index(name) for name in canon] + [len(held), len(held) + 1])
    for i, name in enumerate(canon):
        x = jnp.roll(x, dims[name][3], axis=i)
    return x.reshape(-1, x.shape[-1]), anchor


def level_dims(level, sizes, idx):
    nxa, nya, ngy = sizes
    xa, ya, gy = idx
    dims = {"Z": ("gy", ngy, ngy, gy)}
    if level == 0:
        dims["Y"] = (YA, 2, nya, ya % 2)
    else:
        dims["Y"] = (YA, nya, nya, ya)
    if level == 2:
        dims["X"] = (XA, 2, nxa, xa % 2)
    elif level == 3:
        dims["X"] = (XA, nxa, nxa, xa)
    return dims


ORDERS = {
    0: (("Z", "Y"), ("Y", "Z")),
    1: (("Y", "Z"),),
    2: (("Z", "Y", "X"), ("X", "Z", "Y"), ("Y", "X", "Z")),
    3: (("Z", "Y", "X"), ("X", "Z", "Y"), ("Y", "X", "Z")),
}


def split_columns(front, core, groups):
    rows = front.shape[0]
    four = front.reshape(rows, groups, 2, -1)
    mine = lax.dynamic_index_in_dim(four, core, axis=2, keepdims=False).reshape(rows, -1)
    theirs = lax.dynamic_index_in_dim(four, 1 - core, axis=2, keepdims=False).reshape(rows, -1)
    return mine, moved(theirs, "c", [(0, 1), (1, 0)])


def apply_front(prepare, state, level, sizes, idx):
    dims = level_dims(level, sizes, idx)
    orders = ORDERS[level]
    width = state.shape[1]
    count = len(orders)
    edges = [width * i // count // 128 * 128 for i in range(count)] + [width]
    if level == 0 and count == 2:
        edges = [0, width * 2 // 3 // 128 * 128, width]
    mine = []
    theirs = []
    wholes = []
    anchor = None
    for i, order in enumerate(orders):
        part = state[:, edges[i] : edges[i + 1]]
        whole, got = gather_front(part, dims, order)
        wholes.append(whole)
        anchor = got if anchor is None else anchor
    own_a, other_a = prepare(anchor)
    for whole in wholes:
        mine.append(jnp.dot(own_a, whole, preferred_element_type=jnp.float32))
        theirs.append(jnp.dot(other_a, whole, preferred_element_type=jnp.float32))
    mine = jnp.concatenate(mine, 1)
    theirs = jnp.concatenate(theirs, 1)
    return mine + moved(theirs, "c", [(0, 1), (1, 0)])


def pair_swap(x, axis, size, mask):
    return lax.ppermute(x, axis, [(i, i ^ mask) for i in range(size)])


def spread_front(front, kbits, group, coords):
    rows = front.shape[0]
    names = list(kbits)
    a = front.reshape([rows] + [2] * len(names) + [-1])
    lead = 1
    for axis in group:
        me = coords[axis]
        pos = lead + names.index(axis)
        mine = lax.dynamic_index_in_dim(a, me, axis=pos, keepdims=False)
        theirs = lax.dynamic_index_in_dim(a, 1 - me, axis=pos, keepdims=False)
        got = pair_swap(theirs, axis, 2, 1)
        a = jnp.where(me == 0, jnp.stack([mine, got]), jnp.stack([got, mine]))
        names.remove(axis)
        lead += 1
    return a, names, lead


def doubled(z, steps, coords, sizes):
    cur = z
    for axis, mask, _ in steps:
        got = pair_swap(cur, axis, sizes[axis], mask)
        bit = coords[axis] // mask % 2
        cur = jnp.where(bit == 0, jnp.concatenate([cur, got], 0), jnp.concatenate([got, cur], 0))
    return cur


def apply_grouped(spread, state, steps, group, coords, sizes):
    a, names, lead = spread
    order = [names.index(k) for _, _, k in reversed(steps)]
    perm = list(range(lead)) + [lead + i for i in order] + [lead + len(names)]
    matrix = jnp.transpose(a, perm)
    rows = int(np.prod(matrix.shape[:lead]))
    matrix = matrix.reshape(rows, -1)
    whole = doubled(state, steps, coords, sizes)
    p = jnp.dot(matrix, whole, preferred_element_type=jnp.float32)
    for axis in reversed(group):
        p = p.reshape(2, -1, p.shape[-1])
        me = coords[axis]
        mine = lax.dynamic_index_in_dim(p, me, axis=0, keepdims=False)
        theirs = lax.dynamic_index_in_dim(p, 1 - me, axis=0, keepdims=False)
        p = mine + pair_swap(theirs, axis, 2, 1)
    return p


def padded_2(cells, sides, width):
    for axis, count, dim in sides:
        ends = count - 1
        head = lax.slice_in_dim(cells, 0, width, axis=dim)
        tail = lax.slice_in_dim(cells, cells.shape[dim] - width, cells.shape[dim], axis=dim)
        cells = jnp.concatenate(
            [
                lax.ppermute(tail, axis, [(i, (i + 1) % count) for i in range(ends)]),
                cells,
                lax.ppermute(head, axis, [((i + 1) % count, i) for i in range(ends)]),
            ],
            axis=dim,
        )
    return cells


def make_local(sizes):
    nxa, nya, ngy = sizes
    ngx = nxa * nya * 2
    leaf_bits = ngx.bit_length() - 4

    def local(
        leaf_load,
        front_zero,
        front_one,
        front_two,
        front_root,
        load_one,
        load_two,
        load_root,
        map_one,
        map_two,
        map_root,
        adjoint,
    ):
        fronts = (front_zero, front_one, front_two, front_root)
        loads = (load_one, load_two, load_root)
        mappings = (map_one, map_two, map_root)
        coords = {name: lax.axis_index(name) for name in ALL}
        xa = coords["xh"] * 2 + coords["xl"]
        ya = coords["yh"] * 2 + coords["yl"]
        core = coords["c"]
        row_index = coords["gy"]
        column = (xa * nya + ya) * 2 + core
        idx = (xa, ya, row_index)
        axis_sizes = {name: 2 for name in GX}
        axis_sizes["gy"] = ngy
        gy_bits = [("g%d" % b, 1 << b) for b in reversed(range(ngy.bit_length() - 1))]
        kbits = {
            2: ["xl", "yh", "yl", "c"] + [name for name, _ in gy_bits],
            3: ["xh", "xl", "yh", "yl", "c"] + [name for name, _ in gy_bits],
        }
        high = [("gy",) + tuple(reversed(gy_bits[0]))]
        low = [("gy",) + tuple(reversed(bit)) for bit in gy_bits[1:]]
        steps = {
            2: high + [("yh", 1, "yh")] + low,
            3: high + [("xh", 1, "xh"), ("yh", 1, "yh")] + low,
        }
        parts = {}

        def prepare(anchor):
            tied = lax.optimization_barrier((fronts[0], anchor))[0]
            return split_columns(tied, core, 2)

        def product_of(level, state):
            if level == 0:
                return apply_front(prepare, state, level, sizes, idx)
            if level == 1:
                return apply_front(lambda anchor: parts[1], state, level, sizes, idx)
            return apply_grouped(parts[level], state, steps[level], GROUP, coords, axis_sizes)

        state = leaf_load
        for level in range(3):
            bits = leaf_bits + level
            if level == 2:
                held = (parts[2][0], parts[3][0])
                state, held = lax.optimization_barrier((state, held))
                parts[2] = (held[0],) + parts[2][1:]
                parts[3] = (held[1],) + parts[3][1:]
            product = product_of(level, state)
            if level == 0:
                tied = lax.optimization_barrier((fronts[1:], product))[0]
                parts[1] = split_columns(tied[0], core, nya)
                for later in (2, 3):
                    parts[later] = spread_front(tied[later - 1], kbits[later], GROUP, coords)
            other = moved(product, GX, [(i, i ^ 1 << bits) for i in range(ngx)])
            upper = column >> bits & 1 == 1
            first = jnp.where(upper, other, product)
            second = jnp.where(upper, product, other)
            half = product.shape[0] // 2
            position = column % 2 ** (bits + 1) * ngy + row_index
            local_map = lax.dynamic_slice_in_dim(mappings[level], position * half, half, 0)
            total = (
                loads[level]
                + jnp.take(first, local_map[:, 0], axis=0)
                + jnp.take(second, local_map[:, 1], axis=0)
            )
            state = total.astype(jnp.bfloat16)
        root_solution = product_of(3, state)
        cells_x = adjoint.shape[0]
        cells_y = adjoint.shape[1]
        width = adjoint.shape[2]
        plane = root_solution.reshape(cells_x, cells_y, width)
        stacked = jnp.stack([plane, adjoint])
        padded = padded_2(stacked, ((GX, ngx, 1), ("gy", ngy, 2)), 1)
        padded_u = padded[0]
        padded_a = padded[1]
        gradient = jnp.zeros((cells_x, cells_y, width), jnp.float32)
        for lo_x, lo_y in ((2, 1), (0, 1), (1, 2), (1, 0)):
            near_u = padded_u[lo_x : lo_x + cells_x, lo_y : lo_y + cells_y]
            near_a = padded_a[lo_x : lo_x + cells_x, lo_y : lo_y + cells_y]
            gradient = gradient + (plane - near_u) * (adjoint - near_a)
        return (root_solution, gradient)

    return local


def solution(mesh):
    ngx = mesh.shape["gx"]
    ngy = mesh.shape["gy"]
    nya = 4
    nxa = ngx // (2 * nya)
    devices = np.asarray(mesh.devices).reshape(2, nxa // 2, 2, nya // 2, 2, ngy)
    fine = Mesh(devices, ALL)
    rows = P(ALL, None)
    in_specs = (rows,) * 8 + (P(), P(), P(), P(GX, "gy", None))
    out_specs = (rows, P(GX, "gy", None))
    return jax.shard_map(
        make_local((nxa, nya, ngy)), mesh=fine, in_specs=in_specs, out_specs=out_specs, check_vma=False
    )
```

```python
import numpy as np
import jax
import jax.numpy as jnp
from jax import lax
from jax.sharding import Mesh, PartitionSpec as P

GX = ("xh", "xl", "yh", "yl", "c")
ALL = GX + ("gy",)
YA = ("yh", "yl")
XA = ("xh", "xl")
GROUP = ("xl", "yl", "c")


def moved(x, axis, pairs):
    return lax.ppermute(x, axis, pairs)


def ring_blocks(x, axis, n, size):
    if n == 2 and size != 2:
        got = moved(x, axis, [(i, i ^ 1) for i in range(size)])
        return jnp.stack([x, got]), got
    if n == 4 and size == 4:
        got = moved(x, axis, [(i, i ^ 1) for i in range(size)])
        pair = moved(jnp.stack([x, got]), axis, [(i, i ^ 2) for i in range(size)])
        by_xor = jnp.stack([x, got, pair[0], pair[1]])
        me = lax.axis_index(axis)
        return jnp.take(by_xor, (me + jnp.arange(n)) % n ^ me, axis=0), got
    up = [(i, (i + 1) % n) for i in range(n)]
    down = [(i, (i - 1) % n) for i in range(n)]
    pieces = [None] * n
    pieces[0] = x
    fwd = x
    bwd = x
    for s in range(1, (n - 1) // 2 + 1):
        fwd = moved(fwd, axis, up)
        bwd = moved(bwd, axis, down)
        pieces[n - s] = fwd
        pieces[s] = bwd
    if n % 2 == 0:
        h = x.shape[0] // 2
        a = moved(fwd[:h], axis, up)
        b = moved(bwd[h:], axis, down)
        pieces[n // 2] = jnp.concatenate([a, b], 0)
    return jnp.stack(pieces), pieces[1]


def gather_front(block, dims, order):
    held = []
    x = block
    anchor = None
    for name in order:
        axis, n, size, me = dims[name]
        x, got = ring_blocks(x, axis, n, size)
        anchor = got if anchor is None else anchor
        held.insert(0, name)
    canon = [name for name in ("X", "Y", "Z") if name in dims]
    x = jnp.transpose(x, [held.index(name) for name in canon] + [len(held), len(held) + 1])
    for i, name in enumerate(canon):
        x = jnp.roll(x, dims[name][3], axis=i)
    return x.reshape(-1, x.shape[-1]), anchor


def level_dims(level, sizes, idx):
    nxa, nya, ngy = sizes
    xa, ya, gy = idx
    dims = {"Z": ("gy", ngy, ngy, gy)}
    if level == 0:
        dims["Y"] = (YA, 2, nya, ya % 2)
    else:
        dims["Y"] = (YA, nya, nya, ya)
    if level == 2:
        dims["X"] = (XA, 2, nxa, xa % 2)
    elif level == 3:
        dims["X"] = (XA, nxa, nxa, xa)
    return dims


ORDERS = {
    0: (("Z", "Y"), ("Y", "Z")),
    1: (("Y", "Z"),),
    2: (("Z", "Y", "X"), ("X", "Z", "Y"), ("Y", "X", "Z")),
    3: (("Z", "Y", "X"), ("X", "Z", "Y"), ("Y", "X", "Z")),
}


def split_columns(front, core, groups):
    rows = front.shape[0]
    four = front.reshape(rows, groups, 2, -1)
    mine = lax.dynamic_index_in_dim(four, core, axis=2, keepdims=False).reshape(rows, -1)
    theirs = lax.dynamic_index_in_dim(four, 1 - core, axis=2, keepdims=False).reshape(rows, -1)
    return mine, moved(theirs, "c", [(0, 1), (1, 0)])


def apply_front(prepare, state, level, sizes, idx):
    dims = level_dims(level, sizes, idx)
    orders = ORDERS[level]
    width = state.shape[1]
    count = len(orders)
    edges = [width * i // count // 128 * 128 for i in range(count)] + [width]
    mine = []
    theirs = []
    wholes = []
    anchor = None
    for i, order in enumerate(orders):
        part = state[:, edges[i] : edges[i + 1]]
        whole, got = gather_front(part, dims, order)
        wholes.append(whole)
        anchor = got if anchor is None else anchor
    own_a, other_a = prepare(anchor)
    for whole in wholes:
        mine.append(jnp.dot(own_a, whole, preferred_element_type=jnp.float32))
        theirs.append(jnp.dot(other_a, whole, preferred_element_type=jnp.float32))
    mine = jnp.concatenate(mine, 1)
    theirs = jnp.concatenate(theirs, 1)
    return mine + moved(theirs, "c", [(0, 1), (1, 0)])


def pair_swap(x, axis, size, mask):
    return lax.ppermute(x, axis, [(i, i ^ mask) for i in range(size)])


def spread_front(front, kbits, group, coords):
    rows = front.shape[0]
    names = list(kbits)
    a = front.reshape([rows] + [2] * len(names) + [-1])
    lead = 1
    for axis in group:
        me = coords[axis]
        pos = lead + names.index(axis)
        mine = lax.dynamic_index_in_dim(a, me, axis=pos, keepdims=False)
        theirs = lax.dynamic_index_in_dim(a, 1 - me, axis=pos, keepdims=False)
        got = pair_swap(theirs, axis, 2, 1)
        a = jnp.where(me == 0, jnp.stack([mine, got]), jnp.stack([got, mine]))
        names.remove(axis)
        lead += 1
    return a, names, lead


def doubled(z, steps, coords, sizes):
    cur = z
    for axis, mask, _ in steps:
        got = pair_swap(cur, axis, sizes[axis], mask)
        bit = coords[axis] // mask % 2
        cur = jnp.where(bit == 0, jnp.concatenate([cur, got], 0), jnp.concatenate([got, cur], 0))
    return cur


def apply_grouped(spread, state, steps, group, coords, sizes):
    a, names, lead = spread
    order = [names.index(k) for _, _, k in reversed(steps)]
    perm = list(range(lead)) + [lead + i for i in order] + [lead + len(names)]
    matrix = jnp.transpose(a, perm)
    rows = int(np.prod(matrix.shape[:lead]))
    matrix = matrix.reshape(rows, -1)
    whole = doubled(state, steps, coords, sizes)
    p = jnp.dot(matrix, whole, preferred_element_type=jnp.float32)
    for axis in reversed(group):
        p = p.reshape(2, -1, p.shape[-1])
        me = coords[axis]
        mine = lax.dynamic_index_in_dim(p, me, axis=0, keepdims=False)
        theirs = lax.dynamic_index_in_dim(p, 1 - me, axis=0, keepdims=False)
        p = mine + pair_swap(theirs, axis, 2, 1)
    return p


def padded_2(cells, sides, width):
    for axis, count, dim in sides:
        ends = count - 1
        head = lax.slice_in_dim(cells, 0, width, axis=dim)
        tail = lax.slice_in_dim(cells, cells.shape[dim] - width, cells.shape[dim], axis=dim)
        cells = jnp.concatenate(
            [
                lax.ppermute(tail, axis, [(i, (i + 1) % count) for i in range(ends)]),
                cells,
                lax.ppermute(head, axis, [((i + 1) % count, i) for i in range(ends)]),
            ],
            axis=dim,
        )
    return cells


def make_local(sizes):
    nxa, nya, ngy = sizes
    ngx = nxa * nya * 2
    leaf_bits = ngx.bit_length() - 4

    def local(
        leaf_load,
        front_zero,
        front_one,
        front_two,
        front_root,
        load_one,
        load_two,
        load_root,
        map_one,
        map_two,
        map_root,
        adjoint,
    ):
        fronts = (front_zero, front_one, front_two, front_root)
        loads = (load_one, load_two, load_root)
        mappings = (map_one, map_two, map_root)
        coords = {name: lax.axis_index(name) for name in ALL}
        xa = coords["xh"] * 2 + coords["xl"]
        ya = coords["yh"] * 2 + coords["yl"]
        core = coords["c"]
        row_index = coords["gy"]
        column = (xa * nya + ya) * 2 + core
        idx = (xa, ya, row_index)
        axis_sizes = {name: 2 for name in GX}
        axis_sizes["gy"] = ngy
        gy_bits = [("g%d" % b, 1 << b) for b in reversed(range(ngy.bit_length() - 1))]
        kbits = {
            2: ["xl", "yh", "yl", "c"] + [name for name, _ in gy_bits],
            3: ["xh", "xl", "yh", "yl", "c"] + [name for name, _ in gy_bits],
        }
        high = [("gy",) + tuple(reversed(gy_bits[0]))]
        low = [("gy",) + tuple(reversed(bit)) for bit in gy_bits[1:]]
        steps = {
            2: high + [("yh", 1, "yh")] + low,
            3: high + [("xh", 1, "xh"), ("yh", 1, "yh")] + low,
        }
        parts = {}

        def prepare(anchor):
            tied = lax.optimization_barrier((fronts[0], anchor))[0]
            return split_columns(tied, core, 2)

        def product_of(level, state):
            if level == 0:
                return apply_front(prepare, state, level, sizes, idx)
            if level == 1:
                return apply_front(lambda anchor: parts[1], state, level, sizes, idx)
            return apply_grouped(parts[level], state, steps[level], GROUP, coords, axis_sizes)

        state = leaf_load
        for level in range(3):
            bits = leaf_bits + level
            if level == 2:
                held = (parts[2][0], parts[3][0])
                state, held = lax.optimization_barrier((state, held))
                parts[2] = (held[0],) + parts[2][1:]
                parts[3] = (held[1],) + parts[3][1:]
            product = product_of(level, state)
            if level == 0:
                tied = lax.optimization_barrier((fronts[1:], product))[0]
                parts[1] = split_columns(tied[0], core, nya)
                for later in (2, 3):
                    parts[later] = spread_front(tied[later - 1], kbits[later], GROUP, coords)
            other = moved(product, GX, [(i, i ^ 1 << bits) for i in range(ngx)])
            upper = column >> bits & 1 == 1
            first = jnp.where(upper, other, product)
            second = jnp.where(upper, product, other)
            half = product.shape[0] // 2
            position = column % 2 ** (bits + 1) * ngy + row_index
            local_map = lax.dynamic_slice_in_dim(mappings[level], position * half, half, 0)
            total = (
                loads[level]
                + jnp.take(first, local_map[:, 0], axis=0)
                + jnp.take(second, local_map[:, 1], axis=0)
            )
            state = total.astype(jnp.bfloat16)
        root_solution = product_of(3, state)
        cells_x = adjoint.shape[0]
        cells_y = adjoint.shape[1]
        width = adjoint.shape[2]
        plane = root_solution.reshape(cells_x, cells_y, width)
        stacked = jnp.stack([plane, adjoint])
        padded = padded_2(stacked, ((GX, ngx, 1), ("gy", ngy, 2)), 1)
        padded_u = padded[0]
        padded_a = padded[1]
        gradient = jnp.zeros((cells_x, cells_y, width), jnp.float32)
        for lo_x, lo_y in ((2, 1), (0, 1), (1, 2), (1, 0)):
            near_u = padded_u[lo_x : lo_x + cells_x, lo_y : lo_y + cells_y]
            near_a = padded_a[lo_x : lo_x + cells_x, lo_y : lo_y + cells_y]
            gradient = gradient + (plane - near_u) * (adjoint - near_a)
        return (root_solution, gradient)

    return local


def solution(mesh):
    ngx = mesh.shape["gx"]
    ngy = mesh.shape["gy"]
    nya = 4
    nxa = ngx // (2 * nya)
    devices = np.asarray(mesh.devices).reshape(2, nxa // 2, 2, nya // 2, 2, ngy)
    fine = Mesh(devices, ALL)
    rows = P(ALL, None)
    in_specs = (rows,) * 8 + (P(), P(), P(), P(GX, "gy", None))
    out_specs = (rows, P(GX, "gy", None))
    return jax.shard_map(
        make_local((nxa, nya, ngy)), mesh=fine, in_specs=in_specs, out_specs=out_specs, check_vma=False
    )
```

```python
import numpy as np
import jax
import jax.numpy as jnp
from jax import lax
from jax.sharding import Mesh, PartitionSpec as P

GX = ("xh", "xl", "yh", "yl", "c")
ALL = GX + ("gy",)
YA = ("yh", "yl")
XA = ("xh", "xl")
GROUP = ("xl", "yl", "c")


def moved(x, axis, pairs):
    return lax.ppermute(x, axis, pairs)


def ring_blocks(x, axis, n, size):
    if n == 2 and size != 2:
        got = moved(x, axis, [(i, i ^ 1) for i in range(size)])
        return jnp.stack([x, got]), got
    up = [(i, (i + 1) % n) for i in range(n)]
    down = [(i, (i - 1) % n) for i in range(n)]
    pieces = [None] * n
    pieces[0] = x
    fwd = x
    bwd = x
    for s in range(1, (n - 1) // 2 + 1):
        fwd = moved(fwd, axis, up)
        bwd = moved(bwd, axis, down)
        pieces[n - s] = fwd
        pieces[s] = bwd
    if n % 2 == 0:
        h = x.shape[0] // 2
        a = moved(fwd[:h], axis, up)
        b = moved(bwd[h:], axis, down)
        pieces[n // 2] = jnp.concatenate([a, b], 0)
    return jnp.stack(pieces), pieces[1]


def gather_front(block, dims, order):
    held = []
    x = block
    anchor = None
    for name in order:
        axis, n, size, me = dims[name]
        x, got = ring_blocks(x, axis, n, size)
        anchor = got if anchor is None else anchor
        held.insert(0, name)
    canon = [name for name in ("X", "Y", "Z") if name in dims]
    x = jnp.transpose(x, [held.index(name) for name in canon] + [len(held), len(held) + 1])
    for i, name in enumerate(canon):
        x = jnp.roll(x, dims[name][3], axis=i)
    return x.reshape(-1, x.shape[-1]), anchor


def level_dims(level, sizes, idx):
    nxa, nya, ngy = sizes
    xa, ya, gy = idx
    dims = {"Z": ("gy", ngy, ngy, gy)}
    if level == 0:
        dims["Y"] = (YA, 2, nya, ya % 2)
    else:
        dims["Y"] = (YA, nya, nya, ya)
    if level == 2:
        dims["X"] = (XA, 2, nxa, xa % 2)
    elif level == 3:
        dims["X"] = (XA, nxa, nxa, xa)
    return dims


ORDERS = {
    0: (("Z", "Y"), ("Y", "Z")),
    1: (("Y", "Z"),),
    2: (("Z", "Y", "X"), ("X", "Z", "Y"), ("Y", "X", "Z")),
    3: (("Z", "Y", "X"), ("X", "Z", "Y"), ("Y", "X", "Z")),
}


def split_columns(front, core, groups):
    rows = front.shape[0]
    four = front.reshape(rows, groups, 2, -1)
    mine = lax.dynamic_index_in_dim(four, core, axis=2, keepdims=False).reshape(rows, -1)
    theirs = lax.dynamic_index_in_dim(four, 1 - core, axis=2, keepdims=False).reshape(rows, -1)
    return mine, moved(theirs, "c", [(0, 1), (1, 0)])


def apply_front(prepare, state, level, sizes, idx):
    dims = level_dims(level, sizes, idx)
    orders = ORDERS[level]
    width = state.shape[1]
    count = len(orders)
    edges = [width * i // count // 128 * 128 for i in range(count)] + [width]
    mine = []
    theirs = []
    wholes = []
    anchor = None
    for i, order in enumerate(orders):
        part = state[:, edges[i] : edges[i + 1]]
        whole, got = gather_front(part, dims, order)
        wholes.append(whole)
        anchor = got if anchor is None else anchor
    own_a, other_a = prepare(anchor)
    for whole in wholes:
        mine.append(jnp.dot(own_a, whole, preferred_element_type=jnp.float32))
        theirs.append(jnp.dot(other_a, whole, preferred_element_type=jnp.float32))
    mine = jnp.concatenate(mine, 1)
    theirs = jnp.concatenate(theirs, 1)
    return mine + moved(theirs, "c", [(0, 1), (1, 0)])


def pair_swap(x, axis, size, mask):
    return lax.ppermute(x, axis, [(i, i ^ mask) for i in range(size)])


def spread_front(front, kbits, group, coords):
    rows = front.shape[0]
    names = list(kbits)
    a = front.reshape([rows] + [2] * len(names) + [-1])
    lead = 1
    for axis in group:
        me = coords[axis]
        pos = lead + names.index(axis)
        mine = lax.dynamic_index_in_dim(a, me, axis=pos, keepdims=False)
        theirs = lax.dynamic_index_in_dim(a, 1 - me, axis=pos, keepdims=False)
        got = pair_swap(theirs, axis, 2, 1)
        a = jnp.where(me == 0, jnp.stack([mine, got]), jnp.stack([got, mine]))
        names.remove(axis)
        lead += 1
    return a, names, lead


def doubled(z, steps, coords, sizes):
    cur = z
    for axis, mask, _ in steps:
        got = pair_swap(cur, axis, sizes[axis], mask)
        bit = coords[axis] // mask % 2
        cur = jnp.where(bit == 0, jnp.concatenate([cur, got], 0), jnp.concatenate([got, cur], 0))
    return cur


def apply_grouped(spread, state, steps, group, coords, sizes):
    a, names, lead = spread
    order = [names.index(k) for _, _, k in reversed(steps)]
    perm = list(range(lead)) + [lead + i for i in order] + [lead + len(names)]
    matrix = jnp.transpose(a, perm)
    rows = int(np.prod(matrix.shape[:lead]))
    matrix = matrix.reshape(rows, -1)
    whole = doubled(state, steps, coords, sizes)
    p = jnp.dot(matrix, whole, preferred_element_type=jnp.float32)
    for axis in reversed(group):
        p = p.reshape(2, -1, p.shape[-1])
        me = coords[axis]
        mine = lax.dynamic_index_in_dim(p, me, axis=0, keepdims=False)
        theirs = lax.dynamic_index_in_dim(p, 1 - me, axis=0, keepdims=False)
        p = mine + pair_swap(theirs, axis, 2, 1)
    return p


def padded_2(cells, sides, width):
    for axis, count, dim in sides:
        ends = count - 1
        head = lax.slice_in_dim(cells, 0, width, axis=dim)
        tail = lax.slice_in_dim(cells, cells.shape[dim] - width, cells.shape[dim], axis=dim)
        cells = jnp.concatenate(
            [
                lax.ppermute(tail, axis, [(i, (i + 1) % count) for i in range(ends)]),
                cells,
                lax.ppermute(head, axis, [((i + 1) % count, i) for i in range(ends)]),
            ],
            axis=dim,
        )
    return cells


def make_local(sizes):
    nxa, nya, ngy = sizes
    ngx = nxa * nya * 2
    leaf_bits = ngx.bit_length() - 4

    def local(
        leaf_load,
        front_zero,
        front_one,
        front_two,
        front_root,
        load_one,
        load_two,
        load_root,
        map_one,
        map_two,
        map_root,
        adjoint,
    ):
        fronts = (front_zero, front_one, front_two, front_root)
        loads = (load_one, load_two, load_root)
        mappings = (map_one, map_two, map_root)
        coords = {name: lax.axis_index(name) for name in ALL}
        xa = coords["xh"] * 2 + coords["xl"]
        ya = coords["yh"] * 2 + coords["yl"]
        core = coords["c"]
        row_index = coords["gy"]
        column = (xa * nya + ya) * 2 + core
        idx = (xa, ya, row_index)
        axis_sizes = {name: 2 for name in GX}
        axis_sizes["gy"] = ngy
        gy_bits = [("g%d" % b, 1 << b) for b in reversed(range(ngy.bit_length() - 1))]
        kbits = {
            2: ["xl", "yh", "yl", "c"] + [name for name, _ in gy_bits],
            3: ["xh", "xl", "yh", "yl", "c"] + [name for name, _ in gy_bits],
        }
        high = [("gy",) + tuple(reversed(gy_bits[0]))]
        low = [("gy",) + tuple(reversed(bit)) for bit in gy_bits[1:]]
        steps = {
            2: high + [("yh", 1, "yh")] + low,
            3: high + low + [("xh", 1, "xh"), ("yh", 1, "yh")],
        }
        parts = {}

        def prepare(anchor):
            tied = lax.optimization_barrier((fronts[0], anchor))[0]
            return split_columns(tied, core, 2)

        def product_of(level, state):
            if level == 0:
                return apply_front(prepare, state, level, sizes, idx)
            if level == 1:
                return apply_front(lambda anchor: parts[1], state, level, sizes, idx)
            return apply_grouped(parts[level], state, steps[level], GROUP, coords, axis_sizes)

        state = leaf_load
        for level in range(3):
            bits = leaf_bits + level
            if level == 2:
                held = (parts[2][0], parts[3][0])
                state, held = lax.optimization_barrier((state, held))
                parts[2] = (held[0],) + parts[2][1:]
                parts[3] = (held[1],) + parts[3][1:]
            product = product_of(level, state)
            if level == 0:
                tied = lax.optimization_barrier((fronts[1:], product))[0]
                parts[1] = split_columns(tied[0], core, nya)
                for later in (2, 3):
                    parts[later] = spread_front(tied[later - 1], kbits[later], GROUP, coords)
            other = moved(product, GX, [(i, i ^ 1 << bits) for i in range(ngx)])
            upper = column >> bits & 1 == 1
            first = jnp.where(upper, other, product)
            second = jnp.where(upper, product, other)
            half = product.shape[0] // 2
            position = column % 2 ** (bits + 1) * ngy + row_index
            local_map = lax.dynamic_slice_in_dim(mappings[level], position * half, half, 0)
            total = (
                loads[level]
                + jnp.take(first, local_map[:, 0], axis=0)
                + jnp.take(second, local_map[:, 1], axis=0)
            )
            state = total.astype(jnp.bfloat16)
        root_solution = product_of(3, state)
        cells_x = adjoint.shape[0]
        cells_y = adjoint.shape[1]
        width = adjoint.shape[2]
        plane = root_solution.reshape(cells_x, cells_y, width)
        stacked = jnp.stack([plane, adjoint])
        padded = padded_2(stacked, ((GX, ngx, 1), ("gy", ngy, 2)), 1)
        padded_u = padded[0]
        padded_a = padded[1]
        gradient = jnp.zeros((cells_x, cells_y, width), jnp.float32)
        for lo_x, lo_y in ((2, 1), (0, 1), (1, 2), (1, 0)):
            near_u = padded_u[lo_x : lo_x + cells_x, lo_y : lo_y + cells_y]
            near_a = padded_a[lo_x : lo_x + cells_x, lo_y : lo_y + cells_y]
            gradient = gradient + (plane - near_u) * (adjoint - near_a)
        return (root_solution, gradient)

    return local


def solution(mesh):
    ngx = mesh.shape["gx"]
    ngy = mesh.shape["gy"]
    nya = 4
    nxa = ngx // (2 * nya)
    devices = np.asarray(mesh.devices).reshape(2, nxa // 2, 2, nya // 2, 2, ngy)
    fine = Mesh(devices, ALL)
    rows = P(ALL, None)
    in_specs = (rows,) * 8 + (P(), P(), P(), P(GX, "gy", None))
    out_specs = (rows, P(GX, "gy", None))
    return jax.shard_map(
        make_local((nxa, nya, ngy)), mesh=fine, in_specs=in_specs, out_specs=out_specs, check_vma=False
    )
```
